512 devices in a mesh: grp: 16 (over z), lat: 32 (over y, x, core).
Axes of the slice: x: 4, y: 4, z: 16, core: 2. Of those that a mesh axis runs over, the one named last changes fastest.
Arguments:
- stream: bfloat16 [256, 8192], P('lat'), may hold values from -26 to 26
- batch_index: int32 [256], replicated, may hold values from 0 to 255
- weight: bfloat16 [8192, 65536], P(None, ('grp', 'lat')), may hold values from -0.26516504 to 0.26516504
- enc_bias: float32 [65536], P(('grp', 'lat')), may hold values from -1.5 to 0.5
- dec_bias: float32 [8192], replicated, may hold values from -3 to 3
Outputs:
- weight_grad: bfloat16 [8192, 65536], P(None, ('grp', 'lat'))
- bias_grad: float32 [65536], P(('grp', 'lat'))
- recon_error: bfloat16 [256, 8192], P('lat')
The draws below stay inside these ranges and needn't reach their ends.
All inputs are finite; a program needn't handle non-finite values.
Results may differ from the reference program's by a relative error of at most 0.025.
Values may be sent and summed in bfloat16 or wider, within the bound.
No kernel may reach another device: no remote copies, remote signals or barrier semaphores. Data moves between devices by JAX's collectives and lax.ppermute only.
A program may use at most 64 MiB of HBM per device.

```python
import math
import jax
import jax.numpy as jnp
from jax import lax

D = 8192
LAT_DEV = 128
TOKENS = 256
LATENTS = 65536
RUNS = 512


def draw_stream(key, part):
    level = jnp.arange(TOKENS).astype(jnp.float32) / max(TOKENS - 1, 1)
    growth = jnp.exp(0.5 * math.log(3.0) * level)
    values = jnp.clip(jax.random.normal(key, (TOKENS, D), jnp.float32), -5.0, 5.0)
    return (values * growth[:, None]).astype(jnp.bfloat16)


def draw_weight(key, part):
    first_key, second_key = jax.random.split(key, 2)
    values = jnp.clip(jax.random.normal(first_key, (D, LATENTS), jnp.float32), -6.0, 6.0)
    spread = math.log(2.0)
    level = jnp.arange(LATENTS).astype(jnp.float32) / max(LATENTS - 1, 1)
    growth = jnp.exp(0.5 * math.log(3.0) * level)[None, :]
    column_scale = jnp.exp(jax.random.uniform(second_key, (1, LATENTS), jnp.float32, -spread, spread))
    return (values * column_scale * growth / math.sqrt(D)).astype(jnp.bfloat16)


def plant(values, key, low, high):
    dims = values.shape
    place = [jax.random.randint(jax.random.fold_in(key, axis), (), 0, dims[axis]) for axis in range(len(dims))]
    values = values.at[tuple(place)].set(low)
    longest = dims.index(max(dims))
    place[longest] = (place[longest] + 1) % dims[longest]
    return values.at[tuple(place)].set(high)


def shard_levels(own_key, dims, cuts, smallest, high):
    level, own = 1.0, jax.random.fold_in(own_key, 6)
    for axis_at, shards_of in cuts:
        draws = jnp.exp(jax.random.uniform(jax.random.fold_in(own, axis_at), (shards_of,), jnp.float32, smallest / len(cuts), high / len(cuts)))
        level = level * jnp.repeat(draws, dims[axis_at] // shards_of).reshape([-1 if axis == axis_at else 1 for axis in range(len(dims))])
    return level


def noise(own_key, shape, width, reach, kind=jnp.bfloat16):
    result = width * jax.random.normal(own_key, shape, jnp.float32)
    return jnp.clip(result, min=-reach, max=reach).astype(kind)


def setup_inputs(seed: int = 0) -> dict:
    key_of = jax.random.split(jax.random.key(seed), 6)
    return {
        "stream": draw_stream(jax.random.fold_in(key_of[5], 71), 0),
        "batch_index": plant(jax.random.randint(key_of[1], (TOKENS,), 0, TOKENS), jax.random.fold_in(key_of[1], 1), 0, TOKENS - 1).astype(jnp.int32),
        "weight": draw_weight(jax.random.fold_in(key_of[5], 71), 0),
        "enc_bias": jnp.clip(-1.5 + 2.0 * jax.random.uniform(key_of[3], (LATENTS,), jnp.float32) ** shard_levels(key_of[3], (LATENTS,), ((0, 512),), -0.2, 0.2), -1.5, 0.5),
        "dec_bias": noise(key_of[4], (D,), 0.5, 3.0, jnp.float32),
    }


sharpness = 8.0
penalty = 0.25
epsilon = 1e-06

def run_columns(weight, enc_bias, run):
    start = (run * LAT_DEV).astype(jnp.int32)
    columns = lax.dynamic_slice_in_dim(weight, start, LAT_DEV, 1)
    biases = lax.dynamic_slice_in_dim(enc_bias, start, LAT_DEV, 0)
    return (columns, biases)

def reference(stream, batch_index, weight, enc_bias, dec_bias):
    batch = jnp.take(stream, batch_index, axis=0)
    centered = (batch.astype(jnp.float32) - dec_bias).astype(jnp.bfloat16)
    runs = jnp.arange(RUNS, dtype=jnp.int32)

    def forward_run(centered_rows, run):
        columns, biases = run_columns(weight, enc_bias, run)
        preact = jnp.dot(centered_rows, columns, preferred_element_type=jnp.float32) + biases
        active = (jax.nn.softplus(sharpness * preact) / sharpness).astype(jnp.bfloat16)
        return (columns, preact, active)

    def add_run(running, run):
        columns, preact, active = forward_run(centered, run)
        term = lax.dot_general(active, columns, (((1,), (1,)), ((), ())), preferred_element_type=jnp.float32)
        rounded = lax.optimization_barrier(term.astype(jnp.bfloat16)).astype(jnp.float32)
        return (running + rounded, None)
    summed, _ = lax.scan(add_run, jnp.zeros((TOKENS, D), jnp.float32), runs)
    error = summed + dec_bias - batch.astype(jnp.float32)
    grad_rows = (2.0 * error).astype(jnp.bfloat16)

    def grad_run(run):
        columns, preact, active = forward_run(centered, run)
        grad_active = jnp.dot(grad_rows, columns, preferred_element_type=jnp.float32) + penalty
        grad_pre = grad_active * jax.nn.sigmoid(sharpness * preact)
        grad_raw = lax.dot_general(centered, grad_pre.astype(jnp.bfloat16), (((0,), (0,)), ((), ())), preferred_element_type=jnp.float32)
        grad_raw = grad_raw + lax.dot_general(grad_rows, active, (((0,), (0,)), ((), ())), preferred_element_type=jnp.float32)
        return (grad_raw, lax.optimization_barrier(jnp.sum(grad_pre, axis=0)))

    def add_squares(total, run):
        grad_raw, bias_raw = grad_run(run)
        return (total + jnp.sum(grad_raw * grad_raw) + jnp.sum(bias_raw * bias_raw), bias_raw)
    total_sq, bias_raw = lax.scan(add_squares, jnp.zeros((), jnp.float32), runs)
    factor = jnp.minimum(1.0, 1.0 / jnp.sqrt(total_sq / ((D + 1) * LATENTS) + epsilon))

    def scaled_run(run):
        grad_raw, _ = grad_run(run)
        return (grad_raw * factor).astype(jnp.bfloat16)
    weight_grad = lax.map(scaled_run, runs).transpose(1, 0, 2).reshape(D, LATENTS)
    bias_grad = (bias_raw * factor).reshape(LATENTS)
    return (weight_grad, bias_grad, error.astype(jnp.bfloat16))
```

```python
import jax
import jax.numpy as jnp
from jax import lax
from jax.sharding import PartitionSpec as P

sharpness = 8.0
penalty = 0.25
epsilon = 1e-06


def xor_pairs(n, bit):
    return [(i, i ^ (1 << bit)) for i in range(n)]


def butterfly_sum(x, axis, n, send_dtype):
    acc = x
    for bit in range(n.bit_length() - 1):
        sent = acc.astype(send_dtype)
        acc = sent.astype(jnp.float32) + lax.ppermute(sent, axis, xor_pairs(n, bit)).astype(jnp.float32)
    return acc


def body(stream, batch_index, weight, enc_bias, dec_bias):
    own_rows = stream.shape[0]
    n_lat = lax.axis_size("lat")
    n_grp = lax.axis_size("grp")
    rank_lat = lax.axis_index("lat")
    gathered = lax.all_gather(stream, "lat", axis=0, tiled=True)
    n_rows = gathered.shape[0]
    onehot = (batch_index[:, None] == lax.broadcasted_iota(jnp.int32, (batch_index.shape[0], n_rows), 1)).astype(
        gathered.dtype
    )
    batch = jnp.dot(onehot, gathered, preferred_element_type=jnp.float32).astype(jnp.bfloat16)
    centered = (batch.astype(jnp.float32) - dec_bias).astype(jnp.bfloat16)
    preact = jnp.dot(centered, weight, preferred_element_type=jnp.float32) + enc_bias
    active = (jax.nn.softplus(sharpness * preact) / sharpness).astype(jnp.bfloat16)
    first_row = rank_lat * own_rows
    own_batch = lax.dynamic_slice_in_dim(batch, first_row, own_rows, 0)
    block_recon = lax.psum_scatter(
        lax.dot_general(
            active, weight, (((1,), (1,)), ((), ())), preferred_element_type=jnp.float32
        ).astype(jnp.bfloat16),
        "lat",
        scatter_dimension=0,
        tiled=True,
    )
    recon = butterfly_sum(block_recon.astype(jnp.float32), "grp", n_grp, jnp.bfloat16)
    error_own = recon + dec_bias - own_batch.astype(jnp.float32)
    grad_own = (2.0 * error_own).astype(jnp.bfloat16)
    grad_rows = lax.all_gather(grad_own, "lat", axis=0, tiled=True)
    grad_active = jnp.dot(grad_rows, weight, preferred_element_type=jnp.float32)
    decoder_grad = lax.dot_general(
        grad_rows, active, (((0,), (0,)), ((), ())), preferred_element_type=jnp.float32
    )
    grad_pre = (grad_active + penalty) * jax.nn.sigmoid(sharpness * preact)
    encoder_grad = lax.dot_general(
        centered,
        grad_pre.astype(jnp.bfloat16),
        (((0,), (0,)), ((), ())),
        preferred_element_type=jnp.float32,
    )
    grad_raw = encoder_grad + decoder_grad
    bias_raw = jnp.sum(grad_pre, axis=0)
    local_squares = jnp.sum(grad_raw * grad_raw) + jnp.sum(bias_raw * bias_raw)
    squares = jnp.broadcast_to(local_squares, (1, 128))
    squares = butterfly_sum(squares, "lat", n_lat, jnp.float32)
    total_squares = butterfly_sum(squares, "grp", n_grp, jnp.float32)[0, 0]
    entries = (weight.shape[0] + 1) * weight.shape[1] * n_lat * n_grp
    factor = jnp.minimum(1.0, 1.0 / jnp.sqrt(total_squares / entries + epsilon))
    return (
        (grad_raw * factor).astype(jnp.bfloat16),
        bias_raw * factor,
        error_own.astype(jnp.bfloat16),
    )


def solution(mesh):
    return jax.shard_map(
        body,
        mesh=mesh,
        in_specs=(P("lat", None), P(), P(None, ("grp", "lat")), P(("grp", "lat")), P()),
        out_specs=(P(None, ("grp", "lat")), P(("grp", "lat")), P("lat", None)),
        check_vma=False,
    )
```

```python
import jax
import jax.numpy as jnp
import numpy as np
from jax import lax
from jax.sharding import Mesh
from jax.sharding import PartitionSpec as P

sharpness = 8.0
penalty = 0.25
epsilon = 1e-06

LAT = ("chip", "core")
ALL = ("grp", "chip", "core")


def xor_pairs(n, bit):
    return [(i, i ^ (1 << bit)) for i in range(n)]


def butterfly_sum(x, axis, n, send_dtype):
    acc = x
    for bit in range(n.bit_length() - 1):
        sent = acc.astype(send_dtype)
        acc = sent.astype(jnp.float32) + lax.ppermute(sent, axis, xor_pairs(n, bit)).astype(jnp.float32)
    return acc


def swap_cores(x):
    return lax.ppermute(x, "core", [(0, 1), (1, 0)])


def body(stream, batch_index, weight, enc_bias, dec_bias):
    own_rows = stream.shape[0]
    n_chip = lax.axis_size("chip")
    n_grp = lax.axis_size("grp")
    chip = lax.axis_index("chip")
    core = lax.axis_index("core")
    half = n_chip * own_rows
    n_tok = batch_index.shape[0]

    mine = lax.all_gather(stream, "chip", axis=0, tiled=True)
    gathered = jnp.concatenate([mine, swap_cores(mine)], axis=0)

    q = jnp.arange(n_tok, dtype=jnp.int32)
    side = q // half
    q_chip = (q % half) // own_rows
    q_row = q % own_rows
    q_core = jnp.where(side == 0, core, 1 - core)
    token = (q_chip * 2 + q_core) * own_rows + q_row
    src = jnp.take(batch_index, token)
    s_chip = src // (2 * own_rows)
    s_core = (src // own_rows) % 2
    place = jnp.where(s_core == core, 0, half) + s_chip * own_rows + src % own_rows
    onehot = (place[:, None] == lax.broadcasted_iota(jnp.int32, (n_tok, gathered.shape[0]), 1)).astype(
        gathered.dtype
    )
    batch = jnp.dot(onehot, gathered, preferred_element_type=jnp.float32).astype(jnp.bfloat16)
    centered = (batch.astype(jnp.float32) - dec_bias).astype(jnp.bfloat16)
    preact = jnp.dot(centered, weight, preferred_element_type=jnp.float32) + enc_bias
    active = (jax.nn.softplus(sharpness * preact) / sharpness).astype(jnp.bfloat16)
    own_batch = lax.dynamic_slice_in_dim(batch, chip * own_rows, own_rows, 0)

    partial = lax.dot_general(
        active, weight, (((1,), (1,)), ((), ())), preferred_element_type=jnp.float32
    ).astype(jnp.bfloat16)
    halves = partial.reshape(2, n_chip, own_rows, partial.shape[1])
    by_core = jnp.where(core == 0, halves, halves[::-1])
    lat_order = jnp.swapaxes(by_core, 0, 1).reshape(partial.shape)
    block_recon = lax.psum_scatter(lat_order, LAT, scatter_dimension=0, tiled=True)
    recon = butterfly_sum(block_recon.astype(jnp.float32), "grp", n_grp, jnp.bfloat16)
    error_own = recon + dec_bias - own_batch.astype(jnp.float32)
    grad_own = (2.0 * error_own).astype(jnp.bfloat16)
    grad_mine = lax.all_gather(grad_own, "chip", axis=0, tiled=True)
    grad_rows = jnp.concatenate([grad_mine, swap_cores(grad_mine)], axis=0)

    grad_active = jnp.dot(grad_rows, weight, preferred_element_type=jnp.float32)
    decoder_grad = lax.dot_general(
        grad_rows, active, (((0,), (0,)), ((), ())), preferred_element_type=jnp.float32
    )
    grad_pre = (grad_active + penalty) * jax.nn.sigmoid(sharpness * preact)
    encoder_grad = lax.dot_general(
        centered,
        grad_pre.astype(jnp.bfloat16),
        (((0,), (0,)), ((), ())),
        preferred_element_type=jnp.float32,
    )
    grad_raw = encoder_grad + decoder_grad
    bias_raw = jnp.sum(grad_pre, axis=0)
    local_squares = jnp.sum(grad_raw * grad_raw) + jnp.sum(bias_raw * bias_raw)
    squares = jnp.broadcast_to(local_squares, (1, 128))
    squares = butterfly_sum(squares, "core", 2, jnp.float32)
    squares = butterfly_sum(squares, "chip", n_chip, jnp.float32)
    total_squares = butterfly_sum(squares, "grp", n_grp, jnp.float32)[0, 0]
    entries = (weight.shape[0] + 1) * weight.shape[1] * 2 * n_chip * n_grp
    factor = jnp.minimum(1.0, 1.0 / jnp.sqrt(total_squares / entries + epsilon))
    return (
        (grad_raw * factor).astype(jnp.bfloat16),
        bias_raw * factor,
        error_own.astype(jnp.bfloat16),
    )


def solution(mesh):
    devices = np.asarray(mesh.devices)
    n_grp, n_lat = devices.shape
    split = Mesh(devices.reshape(n_grp, n_lat // 2, 2), ALL)
    return jax.shard_map(
        body,
        mesh=split,
        in_specs=(P(LAT, None), P(), P(None, ALL), P(ALL), P()),
        out_specs=(P(None, ALL), P(ALL), P(LAT, None)),
        check_vma=False,
    )
```

```python
import jax
import jax.numpy as jnp
import numpy as np
from jax import lax
from jax.sharding import PartitionSpec as P

sharpness = 8.0
penalty = 0.25
epsilon = 1e-06


def xor_pairs(n, bit):
    return [(i, i ^ (1 << bit)) for i in range(n)]


def butterfly_sum(x, axis, n, send_dtype):
    acc = x
    for bit in range(n.bit_length() - 1):
        sent = acc.astype(send_dtype)
        acc = sent.astype(jnp.float32) + lax.ppermute(sent, axis, xor_pairs(n, bit)).astype(jnp.float32)
    return acc


LAT_MASKS = (1, 2, 6, 8, 24)


def logical_rank(r):
    b = [(r >> i) & 1 for i in range(5)]
    return (b[0] << 4) | ((b[1] ^ b[2]) << 3) | (b[2] << 2) | ((b[3] ^ b[4]) << 1) | b[4]


def lat_rank_of(p):
    l0, l1, l2, l3, l4 = [(p >> i) & 1 for i in range(5)]
    return l4 | ((l3 ^ l2) << 1) | (l2 << 2) | ((l1 ^ l0) << 3) | (l0 << 4)


def masked_pairs(n, mask):
    return [(i, i ^ mask) for i in range(n)]


def halving_scatter(x, rank, n):
    me = logical_rank(rank)
    acc = x.reshape((n,) + x.shape[1:])
    for j, mask in enumerate(LAT_MASKS):
        bit = (me >> (4 - j)) & 1
        acc = acc.reshape((2, acc.shape[0] // 2) + acc.shape[1:])
        kept = lax.dynamic_index_in_dim(acc, bit, 0, keepdims=False)
        sent = lax.dynamic_index_in_dim(acc, 1 - bit, 0, keepdims=False).astype(jnp.bfloat16)
        acc = kept.astype(jnp.float32) + lax.ppermute(sent, "lat", masked_pairs(n, mask)).astype(jnp.float32)
    return acc[0]


def body(stream, batch_index, weight, enc_bias, dec_bias):
    own_rows = stream.shape[0]
    n_lat = lax.axis_size("lat")
    n_grp = lax.axis_size("grp")
    rank_lat = lax.axis_index("lat")
    gathered = lax.all_gather(stream, "lat", axis=0, tiled=True)
    n_rows = gathered.shape[0]
    onehot = (batch_index[:, None] == lax.broadcasted_iota(jnp.int32, (batch_index.shape[0], n_rows), 1)).astype(
        gathered.dtype
    )
    batch = jnp.dot(onehot, gathered, preferred_element_type=jnp.float32).astype(jnp.bfloat16)
    centered = (batch.astype(jnp.float32) - dec_bias).astype(jnp.bfloat16)
    preact = jnp.dot(centered, weight, preferred_element_type=jnp.float32) + enc_bias
    active = (jax.nn.softplus(sharpness * preact) / sharpness).astype(jnp.bfloat16)
    first_row = rank_lat * own_rows
    own_batch = lax.dynamic_slice_in_dim(batch, first_row, own_rows, 0)
    order = np.array([lat_rank_of(p) for p in range(n_lat)], dtype=np.int32)
    active_log = jnp.take(active.reshape(n_lat, own_rows, -1), order, axis=0).reshape(active.shape)
    partial = lax.dot_general(
        active_log, weight, (((1,), (1,)), ((), ())), preferred_element_type=jnp.float32
    ).astype(jnp.bfloat16)
    block_recon = halving_scatter(partial.reshape(n_lat, own_rows, -1), rank_lat, n_lat)
    recon = butterfly_sum(block_recon.astype(jnp.float32), "grp", n_grp, jnp.bfloat16)
    error_own = recon + dec_bias - own_batch.astype(jnp.float32)
    grad_own = (2.0 * error_own).astype(jnp.bfloat16)
    grad_rows = lax.all_gather(grad_own, "lat", axis=0, tiled=True)
    grad_active = jnp.dot(grad_rows, weight, preferred_element_type=jnp.float32)
    decoder_grad = lax.dot_general(
        grad_rows, active, (((0,), (0,)), ((), ())), preferred_element_type=jnp.float32
    )
    grad_pre = (grad_active + penalty) * jax.nn.sigmoid(sharpness * preact)
    encoder_grad = lax.dot_general(
        centered,
        grad_pre.astype(jnp.bfloat16),
        (((0,), (0,)), ((), ())),
        preferred_element_type=jnp.float32,
    )
    grad_raw = encoder_grad + decoder_grad
    bias_raw = jnp.sum(grad_pre, axis=0)
    local_squares = jnp.sum(grad_raw * grad_raw) + jnp.sum(bias_raw * bias_raw)
    squares = jnp.broadcast_to(local_squares, (1, 128))
    for mask in LAT_MASKS:
        squares = squares + lax.ppermute(squares, "lat", masked_pairs(n_lat, mask))
    total_squares = butterfly_sum(squares, "grp", n_grp, jnp.float32)[0, 0]
    entries = (weight.shape[0] + 1) * weight.shape[1] * n_lat * n_grp
    factor = jnp.minimum(1.0, 1.0 / jnp.sqrt(total_squares / entries + epsilon))
    return (
        (grad_raw * factor).astype(jnp.bfloat16),
        bias_raw * factor,
        error_own.astype(jnp.bfloat16),
    )


def solution(mesh):
    return jax.shard_map(
        body,
        mesh=mesh,
        in_specs=(P("lat", None), P(), P(None, ("grp", "lat")), P(("grp", "lat")), P()),
        out_specs=(P(None, ("grp", "lat")), P(("grp", "lat")), P("lat", None)),
        check_vma=False,
    )
```

```python
import jax
import jax.numpy as jnp
import numpy as np
from jax import lax
from jax.sharding import PartitionSpec as P

sharpness = 8.0
penalty = 0.25
epsilon = 1e-06


def xor_pairs(n, bit):
    return [(i, i ^ (1 << bit)) for i in range(n)]


def butterfly_sum(x, axis, n, send_dtype):
    acc = x
    for bit in range(n.bit_length() - 1):
        sent = acc.astype(send_dtype)
        acc = sent.astype(jnp.float32) + lax.ppermute(sent, axis, xor_pairs(n, bit)).astype(jnp.float32)
    return acc


CORE, X1, X3, Y1, Y3 = 1, 2, 6, 8, 24
LAT_MASKS = (CORE, X1, X3, Y1, Y3)
ORDER_X_FIRST = (CORE, X1, X3, Y1, Y3)
ORDER_Y_FIRST = (CORE, Y1, Y3, X1, X3)


def logical_rank(r, masks):
    coeffs = basis_coefficients(masks)
    out = 0
    for bit in range(5):
        rb = (r >> bit) & 1
        for j in range(5):
            if (coeffs[bit] >> j) & 1:
                out = out ^ (rb << (4 - j))
    return out


def basis_coefficients(masks):
    rows = [(m, 1 << j) for j, m in enumerate(masks)]
    result = []
    for bit in range(5):
        target = 1 << bit
        found = None
        for combo in range(1, 32):
            v = 0
            for j in range(5):
                if (combo >> j) & 1:
                    v ^= rows[j][0]
            if v == target:
                found = combo
                break
        result.append(found)
    return result


def lat_rank_of(p, masks):
    r = 0
    for j, m in enumerate(masks):
        if (p >> (4 - j)) & 1:
            r ^= m
    return r


def masked_pairs(n, mask):
    return [(i, i ^ mask) for i in range(n)]


def halving_scatter(x, rank, n, masks):
    me = logical_rank(rank, masks)
    acc = x
    for j, mask in enumerate(masks):
        bit = (me >> (4 - j)) & 1
        acc = acc.reshape((2, acc.shape[0] // 2) + acc.shape[1:])
        kept = lax.dynamic_index_in_dim(acc, bit, 0, keepdims=False)
        sent = lax.dynamic_index_in_dim(acc, 1 - bit, 0, keepdims=False).astype(jnp.bfloat16)
        acc = kept.astype(jnp.float32) + lax.ppermute(sent, "lat", masked_pairs(n, mask)).astype(jnp.float32)
    return acc[0]


def body(stream, batch_index, weight, enc_bias, dec_bias):
    own_rows = stream.shape[0]
    n_lat = lax.axis_size("lat")
    n_grp = lax.axis_size("grp")
    rank_lat = lax.axis_index("lat")
    gathered = lax.all_gather(stream, "lat", axis=0, tiled=True)
    n_rows = gathered.shape[0]
    onehot = (batch_index[:, None] == lax.broadcasted_iota(jnp.int32, (batch_index.shape[0], n_rows), 1)).astype(
        gathered.dtype
    )
    batch = jnp.dot(onehot, gathered, preferred_element_type=jnp.float32).astype(jnp.bfloat16)
    centered = (batch.astype(jnp.float32) - dec_bias).astype(jnp.bfloat16)
    preact = jnp.dot(centered, weight, preferred_element_type=jnp.float32) + enc_bias
    active = (jax.nn.softplus(sharpness * preact) / sharpness).astype(jnp.bfloat16)
    first_row = rank_lat * own_rows
    own_batch = lax.dynamic_slice_in_dim(batch, first_row, own_rows, 0)
    blocks = active.reshape(n_lat, own_rows, -1)
    cols = weight.shape[0] // 2
    halves = []
    for k, masks in enumerate((ORDER_X_FIRST, ORDER_Y_FIRST)):
        order = np.array([lat_rank_of(p, masks) for p in range(n_lat)], dtype=np.int32)
        rows = jnp.take(blocks, order, axis=0).reshape(active.shape)
        part = lax.dot_general(
            rows, weight[k * cols:(k + 1) * cols], (((1,), (1,)), ((), ())), preferred_element_type=jnp.float32
        ).astype(jnp.bfloat16)
        halves.append(halving_scatter(part.reshape(n_lat, own_rows, cols), rank_lat, n_lat, masks))
    block_recon = jnp.concatenate(halves, axis=1)
    recon = butterfly_sum(block_recon.astype(jnp.float32), "grp", n_grp, jnp.bfloat16)
    error_own = recon + dec_bias - own_batch.astype(jnp.float32)
    grad_own = (2.0 * error_own).astype(jnp.bfloat16)
    grad_rows = lax.all_gather(grad_own, "lat", axis=0, tiled=True)
    grad_active = jnp.dot(grad_rows, weight, preferred_element_type=jnp.float32)
    decoder_grad = lax.dot_general(
        grad_rows, active, (((0,), (0,)), ((), ())), preferred_element_type=jnp.float32
    )
    grad_pre = (grad_active + penalty) * jax.nn.sigmoid(sharpness * preact)
    encoder_grad = lax.dot_general(
        centered,
        grad_pre.astype(jnp.bfloat16),
        (((0,), (0,)), ((), ())),
        preferred_element_type=jnp.float32,
    )
    grad_raw = encoder_grad + decoder_grad
    bias_raw = jnp.sum(grad_pre, axis=0)
    local_squares = jnp.sum(grad_raw * grad_raw) + jnp.sum(bias_raw * bias_raw)
    squares = jnp.broadcast_to(local_squares, (1, 128))
    for mask in LAT_MASKS:
        squares = squares + lax.ppermute(squares, "lat", masked_pairs(n_lat, mask))
    total_squares = butterfly_sum(squares, "grp", n_grp, jnp.float32)[0, 0]
    entries = (weight.shape[0] + 1) * weight.shape[1] * n_lat * n_grp
    factor = jnp.minimum(1.0, 1.0 / jnp.sqrt(total_squares / entries + epsilon))
    return (
        (grad_raw * factor).astype(jnp.bfloat16),
        bias_raw * factor,
        error_own.astype(jnp.bfloat16),
    )


def solution(mesh):
    return jax.shard_map(
        body,
        mesh=mesh,
        in_specs=(P("lat", None), P(), P(None, ("grp", "lat")), P(("grp", "lat")), P()),
        out_specs=(P(None, ("grp", "lat")), P(("grp", "lat")), P("lat", None)),
        check_vma=False,
    )
```

```python
import jax
import jax.numpy as jnp
import numpy as np
from jax import lax
from jax.sharding import PartitionSpec as P

sharpness = 8.0
penalty = 0.25
epsilon = 1e-06


def xor_pairs(n, bit):
    return [(i, i ^ (1 << bit)) for i in range(n)]


def butterfly_sum(x, axis, n, send_dtype):
    acc = x
    for bit in range(n.bit_length() - 1):
        sent = acc.astype(send_dtype)
        acc = sent.astype(jnp.float32) + lax.ppermute(sent, axis, xor_pairs(n, bit)).astype(jnp.float32)
    return acc


CORE, X1, X3, Y1, Y3 = 1, 2, 6, 8, 24
LAT_MASKS = (CORE, X1, X3, Y1, Y3)
ORDER_X_FIRST = (CORE, X1, X3, Y1, Y3)
ORDER_Y_FIRST = (CORE, Y1, Y3, X1, X3)


def logical_rank(r, masks):
    coeffs = basis_coefficients(masks)
    out = 0
    for bit in range(5):
        rb = (r >> bit) & 1
        for j in range(5):
            if (coeffs[bit] >> j) & 1:
                out = out ^ (rb << (4 - j))
    return out


def basis_coefficients(masks):
    rows = [(m, 1 << j) for j, m in enumerate(masks)]
    result = []
    for bit in range(5):
        target = 1 << bit
        found = None
        for combo in range(1, 32):
            v = 0
            for j in range(5):
                if (combo >> j) & 1:
                    v ^= rows[j][0]
            if v == target:
                found = combo
                break
        result.append(found)
    return result


def lat_rank_of(p, masks):
    r = 0
    for j, m in enumerate(masks):
        if (p >> (4 - j)) & 1:
            r ^= m
    return r


def masked_pairs(n, mask):
    return [(i, i ^ mask) for i in range(n)]


def halving_scatter(x, rank, n, masks):
    me = logical_rank(rank, masks)
    acc = x
    for j, mask in enumerate(masks):
        bit = (me >> (4 - j)) & 1
        acc = acc.reshape((2, acc.shape[0] // 2) + acc.shape[1:])
        kept = lax.dynamic_index_in_dim(acc, bit, 0, keepdims=False)
        sent = lax.dynamic_index_in_dim(acc, 1 - bit, 0, keepdims=False).astype(jnp.bfloat16)
        acc = kept.astype(jnp.float32) + lax.ppermute(sent, "lat", masked_pairs(n, mask)).astype(jnp.float32)
    return acc[0]


def doubling_gather(x, rank, n, masks):
    me = logical_rank(rank, masks)
    acc = x[None]
    for j in reversed(range(len(masks))):
        bit = (me >> (4 - j)) & 1
        got = lax.ppermute(acc, "lat", masked_pairs(n, masks[j]))
        pair = jnp.stack([acc, got])
        acc = jnp.where(bit == 0, pair, pair[::-1]).reshape((2 * acc.shape[0],) + acc.shape[1:])
    order = np.array([logical_rank(r, masks) for r in range(n)], dtype=np.int32)
    return jnp.take(acc, order, axis=0)


def lat_gather(x, rank, n):
    cols = x.shape[1] // 2
    parts = [
        doubling_gather(x[:, k * cols:(k + 1) * cols], rank, n, masks)
        for k, masks in enumerate((ORDER_X_FIRST, ORDER_Y_FIRST))
    ]
    return jnp.concatenate(parts, axis=2).reshape(n * x.shape[0], x.shape[1])


def body(stream, batch_index, weight, enc_bias, dec_bias):
    own_rows = stream.shape[0]
    n_lat = lax.axis_size("lat")
    n_grp = lax.axis_size("grp")
    rank_lat = lax.axis_index("lat")
    gathered = lat_gather(stream, rank_lat, n_lat)
    n_rows = gathered.shape[0]
    onehot = (batch_index[:, None] == lax.broadcasted_iota(jnp.int32, (batch_index.shape[0], n_rows), 1)).astype(
        gathered.dtype
    )
    batch = jnp.dot(onehot, gathered, preferred_element_type=jnp.float32).astype(jnp.bfloat16)
    centered = (batch.astype(jnp.float32) - dec_bias).astype(jnp.bfloat16)
    preact = jnp.dot(centered, weight, preferred_element_type=jnp.float32) + enc_bias
    active = (jax.nn.softplus(sharpness * preact) / sharpness).astype(jnp.bfloat16)
    first_row = rank_lat * own_rows
    own_batch = lax.dynamic_slice_in_dim(batch, first_row, own_rows, 0)
    blocks = active.reshape(n_lat, own_rows, -1)
    cols = weight.shape[0] // 2
    halves = []
    for k, masks in enumerate((ORDER_X_FIRST, ORDER_Y_FIRST)):
        order = np.array([lat_rank_of(p, masks) for p in range(n_lat)], dtype=np.int32)
        rows = jnp.take(blocks, order, axis=0).reshape(active.shape)
        part = lax.dot_general(
            rows, weight[k * cols:(k + 1) * cols], (((1,), (1,)), ((), ())), preferred_element_type=jnp.float32
        ).astype(jnp.bfloat16)
        halves.append(halving_scatter(part.reshape(n_lat, own_rows, cols), rank_lat, n_lat, masks))
    block_recon = jnp.concatenate(halves, axis=1)
    recon = butterfly_sum(block_recon.astype(jnp.float32), "grp", n_grp, jnp.bfloat16)
    error_own = recon + dec_bias - own_batch.astype(jnp.float32)
    grad_own = (2.0 * error_own).astype(jnp.bfloat16)
    grad_rows = lat_gather(grad_own, rank_lat, n_lat)
    grad_active = jnp.dot(grad_rows, weight, preferred_element_type=jnp.float32)
    decoder_grad = lax.dot_general(
        grad_rows, active, (((0,), (0,)), ((), ())), preferred_element_type=jnp.float32
    )
    grad_pre = (grad_active + penalty) * jax.nn.sigmoid(sharpness * preact)
    encoder_grad = lax.dot_general(
        centered,
        grad_pre.astype(jnp.bfloat16),
        (((0,), (0,)), ((), ())),
        preferred_element_type=jnp.float32,
    )
    grad_raw = encoder_grad + decoder_grad
    bias_raw = jnp.sum(grad_pre, axis=0)
    local_squares = jnp.sum(grad_raw * grad_raw) + jnp.sum(bias_raw * bias_raw)
    squares = jnp.broadcast_to(local_squares, (1, 128))
    for mask in LAT_MASKS:
        squares = squares + lax.ppermute(squares, "lat", masked_pairs(n_lat, mask))
    total_squares = butterfly_sum(squares, "grp", n_grp, jnp.float32)[0, 0]
    entries = (weight.shape[0] + 1) * weight.shape[1] * n_lat * n_grp
    factor = jnp.minimum(1.0, 1.0 / jnp.sqrt(total_squares / entries + epsilon))
    return (
        (grad_raw * factor).astype(jnp.bfloat16),
        bias_raw * factor,
        error_own.astype(jnp.bfloat16),
    )


def solution(mesh):
    return jax.shard_map(
        body,
        mesh=mesh,
        in_specs=(P("lat", None), P(), P(None, ("grp", "lat")), P(("grp", "lat")), P()),
        out_specs=(P(None, ("grp", "lat")), P(("grp", "lat")), P("lat", None)),
        check_vma=False,
    )
```

```python
import jax
import jax.numpy as jnp
import numpy as np
from jax import lax
from jax.sharding import PartitionSpec as P

sharpness = 8.0
penalty = 0.25
epsilon = 1e-06


def butterfly_sum(x, axis, n, send_dtype, masks):
    acc = x
    for mask in masks:
        sent = acc.astype(send_dtype)
        acc = sent.astype(jnp.float32) + lax.ppermute(sent, axis, masked_pairs(n, mask)).astype(jnp.float32)
    return acc


CORE, X1, X3, Y1, Y3 = 1, 2, 6, 8, 24
LAT_MASKS = (CORE, X1, X3, Y1, Y3)
ORDER_X_FIRST = (CORE, X1, X3, Y1, Y3)
ORDER_Y_FIRST = (CORE, Y1, Y3, X1, X3)
ORDERS = (ORDER_X_FIRST, ORDER_Y_FIRST)
GRP_MASKS = (1, 2, 4, 12)


def logical_rank(r, masks):
    coeffs = basis_coefficients(masks)
    out = 0
    for bit in range(5):
        rb = (r >> bit) & 1
        for j in range(5):
            if (coeffs[bit] >> j) & 1:
                out = out ^ (rb << (4 - j))
    return out


def basis_coefficients(masks):
    rows = [(m, 1 << j) for j, m in enumerate(masks)]
    result = []
    for bit in range(5):
        target = 1 << bit
        found = None
        for combo in range(1, 32):
            v = 0
            for j in range(5):
                if (combo >> j) & 1:
                    v ^= rows[j][0]
            if v == target:
                found = combo
                break
        result.append(found)
    return result


def lat_rank_of(p, masks):
    r = 0
    for j, m in enumerate(masks):
        if (p >> (4 - j)) & 1:
            r ^= m
    return r


def masked_pairs(n, mask):
    return [(i, i ^ mask) for i in range(n)]


def halving_scatter(x, rank, n, masks):
    me = logical_rank(rank, masks)
    acc = x
    for j, mask in enumerate(masks):
        bit = (me >> (4 - j)) & 1
        acc = acc.reshape((2, acc.shape[0] // 2) + acc.shape[1:])
        kept = lax.dynamic_index_in_dim(acc, bit, 0, keepdims=False)
        sent = lax.dynamic_index_in_dim(acc, 1 - bit, 0, keepdims=False).astype(jnp.bfloat16)
        acc = kept.astype(jnp.float32) + lax.ppermute(sent, "lat", masked_pairs(n, mask)).astype(jnp.float32)
    return acc[0]


def doubling_gather(x, rank, n, masks):
    me = logical_rank(rank, masks)
    acc = x[None]
    for j in reversed(range(len(masks))):
        bit = (me >> (4 - j)) & 1
        got = lax.ppermute(acc, "lat", masked_pairs(n, masks[j]))
        pair = jnp.stack([acc, got])
        acc = jnp.where(bit == 0, pair, pair[::-1]).reshape((2 * acc.shape[0],) + acc.shape[1:])
    return acc


def column_halves(x, rank, n):
    cols = x.shape[1] // 2
    return [doubling_gather(x[:, k * cols:(k + 1) * cols], rank, n, masks) for k, masks in enumerate(ORDERS)]


def block_perm(src_masks, dst_masks, n):
    return np.array([logical_rank(lat_rank_of(p, dst_masks), src_masks) for p in range(n)], dtype=np.int32)


def take_blocks(x, perm, rows):
    return jnp.take(x.reshape((len(perm), rows) + x.shape[1:]), perm, axis=0).reshape(x.shape)


def body(stream, batch_index, weight, enc_bias, dec_bias):
    own_rows = stream.shape[0]
    n_lat = lax.axis_size("lat")
    n_grp = lax.axis_size("grp")
    rank_lat = lax.axis_index("lat")
    n_tok = batch_index.shape[0]
    cols = weight.shape[0] // 2
    order_a, order_b = ORDERS
    token_of_row = np.array(
        [lat_rank_of(i // own_rows, order_a) * own_rows + i % own_rows for i in range(n_tok)], dtype=np.int32
    )
    src = jnp.take(batch_index, token_of_row)
    stream_halves = column_halves(stream, rank_lat, n_lat)
    batch_halves = []
    for masks, rows in zip(ORDERS, stream_halves):
        place = logical_rank(src // own_rows, masks) * own_rows + src % own_rows
        onehot = (place[:, None] == lax.broadcasted_iota(jnp.int32, (n_tok, n_tok), 1)).astype(rows.dtype)
        batch_halves.append(
            jnp.dot(onehot, rows.reshape(n_tok, cols), preferred_element_type=jnp.float32).astype(jnp.bfloat16)
        )
    batch = jnp.concatenate(batch_halves, axis=1)
    centered = (batch.astype(jnp.float32) - dec_bias).astype(jnp.bfloat16)
    preact = jnp.dot(centered, weight, preferred_element_type=jnp.float32) + enc_bias
    active = (jax.nn.softplus(sharpness * preact) / sharpness).astype(jnp.bfloat16)
    own_block = logical_rank(rank_lat, order_a)
    own_batch = lax.dynamic_slice_in_dim(batch, own_block * own_rows, own_rows, 0)
    active_b = take_blocks(active, block_perm(order_a, order_b, n_lat), own_rows)
    halves = []
    for k, (masks, rows) in enumerate(zip(ORDERS, (active, active_b))):
        part = lax.dot_general(
            rows, weight[k * cols:(k + 1) * cols], (((1,), (1,)), ((), ())), preferred_element_type=jnp.float32
        ).astype(jnp.bfloat16)
        halves.append(halving_scatter(part.reshape(n_lat, own_rows, cols), rank_lat, n_lat, masks))
    block_recon = jnp.concatenate(halves, axis=1)
    recon = butterfly_sum(block_recon.astype(jnp.float32), "grp", n_grp, jnp.bfloat16, GRP_MASKS)
    error_own = recon + dec_bias - own_batch.astype(jnp.float32)
    grad_own = (2.0 * error_own).astype(jnp.bfloat16)
    grad_a, grad_b = [g.reshape(n_tok, cols) for g in column_halves(grad_own, rank_lat, n_lat)]
    active_part_b = jnp.dot(grad_b, weight[cols:], preferred_element_type=jnp.float32)
    grad_active = jnp.dot(grad_a, weight[:cols], preferred_element_type=jnp.float32) + take_blocks(
        active_part_b, block_perm(order_b, order_a, n_lat), own_rows
    )
    decoder_grad = jnp.concatenate(
        [
            lax.dot_general(g, a, (((0,), (0,)), ((), ())), preferred_element_type=jnp.float32)
            for g, a in ((grad_a, active), (grad_b, active_b))
        ],
        axis=0,
    )
    grad_pre = (grad_active + penalty) * jax.nn.sigmoid(sharpness * preact)
    encoder_grad = lax.dot_general(
        centered,
        grad_pre.astype(jnp.bfloat16),
        (((0,), (0,)), ((), ())),
        preferred_element_type=jnp.float32,
    )
    grad_raw = encoder_grad + decoder_grad
    bias_raw = jnp.sum(grad_pre, axis=0)
    local_squares = jnp.sum(grad_raw * grad_raw) + jnp.sum(bias_raw * bias_raw)
    squares = jnp.broadcast_to(local_squares, (1, 128))
    for mask in LAT_MASKS:
        squares = squares + lax.ppermute(squares, "lat", masked_pairs(n_lat, mask))
    total_squares = butterfly_sum(squares, "grp", n_grp, jnp.float32, GRP_MASKS)[0, 0]
    entries = (weight.shape[0] + 1) * weight.shape[1] * n_lat * n_grp
    factor = jnp.minimum(1.0, 1.0 / jnp.sqrt(total_squares / entries + epsilon))
    return (
        (grad_raw * factor).astype(jnp.bfloat16),
        bias_raw * factor,
        error_own.astype(jnp.bfloat16),
    )


def solution(mesh):
    return jax.shard_map(
        body,
        mesh=mesh,
        in_specs=(P("lat", None), P(), P(None, ("grp", "lat")), P(("grp", "lat")), P()),
        out_specs=(P(None, ("grp", "lat")), P(("grp", "lat")), P("lat", None)),
        check_vma=False,
    )
```

```python
import jax
import jax.numpy as jnp
import numpy as np
from jax import lax
from jax.sharding import PartitionSpec as P

sharpness = 8.0
penalty = 0.25
epsilon = 1e-06


def butterfly_sum(x, axis, n, send_dtype, masks):
    acc = x
    for mask in masks:
        sent = acc.astype(send_dtype)
        acc = sent.astype(jnp.float32) + lax.ppermute(sent, axis, masked_pairs(n, mask)).astype(jnp.float32)
    return acc


def quad_sum(x, axis, n, send_dtype, pairs):
    acc = x
    for masks in pairs:
        sent = acc.astype(send_dtype)
        if len(masks) == 1:
            acc = sent.astype(jnp.float32) + lax.ppermute(sent, axis, masked_pairs(n, masks[0])).astype(jnp.float32)
            continue
        m1, m2 = masks
        a, b, c = [lax.ppermute(sent, axis, masked_pairs(n, m)).astype(jnp.float32) for m in (m1, m2, m1 ^ m2)]
        acc = (sent.astype(jnp.float32) + a) + (b + c)
    return acc


CORE, X1, X3, Y1, Y3 = 1, 2, 6, 8, 24
LAT_MASKS = (CORE, X1, X3, Y1, Y3)
ORDER_X_FIRST = (CORE, X1, X3, Y1, Y3)
ORDER_Y_FIRST = (CORE, Y1, Y3, X1, X3)
ORDERS = (ORDER_X_FIRST, ORDER_Y_FIRST)
GRP_MASKS = (1, 2, 4, 12)
GRP_QUADS = ((1, 2), (4, 12))
LAT_QUADS = ((CORE, X1), (X3, Y1), (Y3,))


def logical_rank(r, masks):
    coeffs = basis_coefficients(masks)
    out = 0
    for bit in range(5):
        rb = (r >> bit) & 1
        for j in range(5):
            if (coeffs[bit] >> j) & 1:
                out = out ^ (rb << (4 - j))
    return out


def basis_coefficients(masks):
    rows = [(m, 1 << j) for j, m in enumerate(masks)]
    result = []
    for bit in range(5):
        target = 1 << bit
        found = None
        for combo in range(1, 32):
            v = 0
            for j in range(5):
                if (combo >> j) & 1:
                    v ^= rows[j][0]
            if v == target:
                found = combo
                break
        result.append(found)
    return result


def lat_rank_of(p, masks):
    r = 0
    for j, m in enumerate(masks):
        if (p >> (4 - j)) & 1:
            r ^= m
    return r


def masked_pairs(n, mask):
    return [(i, i ^ mask) for i in range(n)]


def halving_scatter(x, rank, n, masks):
    me = logical_rank(rank, masks)
    acc = x
    for j, mask in enumerate(masks):
        bit = (me >> (4 - j)) & 1
        acc = acc.reshape((2, acc.shape[0] // 2) + acc.shape[1:])
        kept = lax.dynamic_index_in_dim(acc, bit, 0, keepdims=False)
        sent = lax.dynamic_index_in_dim(acc, 1 - bit, 0, keepdims=False).astype(jnp.bfloat16)
        acc = kept.astype(jnp.float32) + lax.ppermute(sent, "lat", masked_pairs(n, mask)).astype(jnp.float32)
    return acc[0]


def doubling_gather(x, rank, n, masks):
    me = logical_rank(rank, masks)
    acc = x[None]
    for j in reversed(range(len(masks))):
        bit = (me >> (4 - j)) & 1
        got = lax.ppermute(acc, "lat", masked_pairs(n, masks[j]))
        pair = jnp.stack([acc, got])
        acc = jnp.where(bit == 0, pair, pair[::-1]).reshape((2 * acc.shape[0],) + acc.shape[1:])
    return acc


def column_halves(x, rank, n):
    cols = x.shape[1] // 2
    return [doubling_gather(x[:, k * cols:(k + 1) * cols], rank, n, masks) for k, masks in enumerate(ORDERS)]


def block_perm(src_masks, dst_masks, n):
    return np.array([logical_rank(lat_rank_of(p, dst_masks), src_masks) for p in range(n)], dtype=np.int32)


def take_blocks(x, perm, rows):
    return jnp.take(x.reshape((len(perm), rows) + x.shape[1:]), perm, axis=0).reshape(x.shape)


def body(stream, batch_index, weight, enc_bias, dec_bias):
    own_rows = stream.shape[0]
    n_lat = lax.axis_size("lat")
    n_grp = lax.axis_size("grp")
    rank_lat = lax.axis_index("lat")
    n_tok = batch_index.shape[0]
    cols = weight.shape[0] // 2
    order_a, order_b = ORDERS
    token_of_row = np.array(
        [lat_rank_of(i // own_rows, order_a) * own_rows + i % own_rows for i in range(n_tok)], dtype=np.int32
    )
    src = jnp.take(batch_index, token_of_row)
    stream_halves = column_halves(stream, rank_lat, n_lat)
    batch_halves = []
    for masks, rows in zip(ORDERS, stream_halves):
        place = logical_rank(src // own_rows, masks) * own_rows + src % own_rows
        onehot = (place[:, None] == lax.broadcasted_iota(jnp.int32, (n_tok, n_tok), 1)).astype(rows.dtype)
        batch_halves.append(
            jnp.dot(onehot, rows.reshape(n_tok, cols), preferred_element_type=jnp.float32).astype(jnp.bfloat16)
        )
    batch = jnp.concatenate(batch_halves, axis=1)
    centered = (batch.astype(jnp.float32) - dec_bias).astype(jnp.bfloat16)
    preact = jnp.dot(centered, weight, preferred_element_type=jnp.float32) + enc_bias
    active = (jax.nn.softplus(sharpness * preact) / sharpness).astype(jnp.bfloat16)
    own_block = logical_rank(rank_lat, order_a)
    own_batch = lax.dynamic_slice_in_dim(batch, own_block * own_rows, own_rows, 0)
    active_b = take_blocks(active, block_perm(order_a, order_b, n_lat), own_rows)
    halves = []
    for k, (masks, rows) in enumerate(zip(ORDERS, (active, active_b))):
        part = lax.dot_general(
            rows, weight[k * cols:(k + 1) * cols], (((1,), (1,)), ((), ())), preferred_element_type=jnp.float32
        ).astype(jnp.bfloat16)
        halves.append(halving_scatter(part.reshape(n_lat, own_rows, cols), rank_lat, n_lat, masks))
    block_recon = jnp.concatenate(halves, axis=1)
    recon = quad_sum(block_recon.astype(jnp.float32), "grp", n_grp, jnp.bfloat16, GRP_QUADS)
    error_own = recon + dec_bias - own_batch.astype(jnp.float32)
    grad_own = (2.0 * error_own).astype(jnp.bfloat16)
    grad_a, grad_b = [g.reshape(n_tok, cols) for g in column_halves(grad_own, rank_lat, n_lat)]
    active_part_b = jnp.dot(grad_b, weight[cols:], preferred_element_type=jnp.float32)
    grad_active = jnp.dot(grad_a, weight[:cols], preferred_element_type=jnp.float32) + take_blocks(
        active_part_b, block_perm(order_b, order_a, n_lat), own_rows
    )
    decoder_grad = jnp.concatenate(
        [
            lax.dot_general(g, a, (((0,), (0,)), ((), ())), preferred_element_type=jnp.float32)
            for g, a in ((grad_a, active), (grad_b, active_b))
        ],
        axis=0,
    )
    grad_pre = (grad_active + penalty) * jax.nn.sigmoid(sharpness * preact)
    encoder_grad = lax.dot_general(
        centered,
        grad_pre.astype(jnp.bfloat16),
        (((0,), (0,)), ((), ())),
        preferred_element_type=jnp.float32,
    )
    grad_raw = encoder_grad + decoder_grad
    bias_raw = jnp.sum(grad_pre, axis=0)
    local_squares = jnp.sum(grad_raw * grad_raw) + jnp.sum(bias_raw * bias_raw)
    squares = jnp.broadcast_to(local_squares, (1, 128))
    squares = quad_sum(squares, "lat", n_lat, jnp.float32, LAT_QUADS)
    total_squares = quad_sum(squares, "grp", n_grp, jnp.float32, GRP_QUADS)[0, 0]
    entries = (weight.shape[0] + 1) * weight.shape[1] * n_lat * n_grp
    factor = jnp.minimum(1.0, 1.0 / jnp.sqrt(total_squares / entries + epsilon))
    return (
        (grad_raw * factor).astype(jnp.bfloat16),
        bias_raw * factor,
        error_own.astype(jnp.bfloat16),
    )


def solution(mesh):
    return jax.shard_map(
        body,
        mesh=mesh,
        in_specs=(P("lat", None), P(), P(None, ("grp", "lat")), P(("grp", "lat")), P()),
        out_specs=(P(None, ("grp", "lat")), P(("grp", "lat")), P("lat", None)),
        check_vma=False,
    )
```

```python
import jax
import jax.numpy as jnp
import numpy as np
from jax import lax
from jax.sharding import PartitionSpec as P

sharpness = 8.0
penalty = 0.25
epsilon = 1e-06


def butterfly_sum(x, axis, n, send_dtype, masks):
    acc = x
    for mask in masks:
        sent = acc.astype(send_dtype)
        acc = sent.astype(jnp.float32) + lax.ppermute(sent, axis, masked_pairs(n, mask)).astype(jnp.float32)
    return acc


CORE, X1, X3, Y1, Y3 = 1, 2, 6, 8, 24
LAT_MASKS = (CORE, X1, X3, Y1, Y3)
ORDER_X_FIRST = (CORE, X1, X3, Y1, Y3)
ORDER_Y_FIRST = (CORE, Y1, Y3, X1, X3)
ORDERS = (ORDER_X_FIRST, ORDER_Y_FIRST)
GRP_MASKS = (1, 2, 4, 12)


def logical_rank(r, masks):
    coeffs = basis_coefficients(masks)
    out = 0
    for bit in range(5):
        rb = (r >> bit) & 1
        for j in range(5):
            if (coeffs[bit] >> j) & 1:
                out = out ^ (rb << (4 - j))
    return out


def basis_coefficients(masks):
    rows = [(m, 1 << j) for j, m in enumerate(masks)]
    result = []
    for bit in range(5):
        target = 1 << bit
        found = None
        for combo in range(1, 32):
            v = 0
            for j in range(5):
                if (combo >> j) & 1:
                    v ^= rows[j][0]
            if v == target:
                found = combo
                break
        result.append(found)
    return result


def lat_rank_of(p, masks):
    r = 0
    for j, m in enumerate(masks):
        r = r ^ (((p >> (4 - j)) & 1) * m)
    return r


def masked_pairs(n, mask):
    return [(i, i ^ mask) for i in range(n)]


def halving_scatter(x, n, masks):
    acc = x
    for mask in masks:
        acc = acc.reshape((2, acc.shape[0] // 2) + acc.shape[1:])
        sent = acc[1].astype(jnp.bfloat16)
        acc = acc[0].astype(jnp.float32) + lax.ppermute(sent, "lat", masked_pairs(n, mask)).astype(jnp.float32)
    return acc[0]


def doubling_gather(x, n, masks):
    acc = x[None]
    for mask in reversed(masks):
        acc = jnp.concatenate([acc, lax.ppermute(acc, "lat", masked_pairs(n, mask))], axis=0)
    return acc


def column_halves(x, n):
    cols = x.shape[1] // 2
    return [doubling_gather(x[:, k * cols:(k + 1) * cols], n, masks) for k, masks in enumerate(ORDERS)]


def take_blocks(x, perm, rows):
    return jnp.take(x.reshape((perm.shape[0], rows) + x.shape[1:]), perm, axis=0).reshape(x.shape)


def body(stream, batch_index, weight, enc_bias, dec_bias):
    own_rows = stream.shape[0]
    n_lat = lax.axis_size("lat")
    n_grp = lax.axis_size("grp")
    rank_lat = lax.axis_index("lat")
    n_tok = batch_index.shape[0]
    cols = weight.shape[0] // 2
    order_a, order_b = ORDERS
    me_a = logical_rank(rank_lat, order_a)
    me_b = logical_rank(rank_lat, order_b)
    blk = jnp.arange(n_lat, dtype=jnp.int32)
    row = jnp.arange(n_tok, dtype=jnp.int32)
    token_of_row = lat_rank_of(row // own_rows ^ me_a, order_a) * own_rows + row % own_rows
    src = jnp.take(batch_index, token_of_row)
    stream_halves = column_halves(stream, n_lat)
    batch_halves = []
    for masks, me, rows in zip(ORDERS, (me_a, me_b), stream_halves):
        place = (logical_rank(src // own_rows, masks) ^ me) * own_rows + src % own_rows
        onehot = (place[:, None] == lax.broadcasted_iota(jnp.int32, (n_tok, n_tok), 1)).astype(rows.dtype)
        batch_halves.append(
            jnp.dot(onehot, rows.reshape(n_tok, cols), preferred_element_type=jnp.float32).astype(jnp.bfloat16)
        )
    batch = jnp.concatenate(batch_halves, axis=1)
    centered = (batch.astype(jnp.float32) - dec_bias).astype(jnp.bfloat16)
    preact = jnp.dot(centered, weight, preferred_element_type=jnp.float32) + enc_bias
    active = (jax.nn.softplus(sharpness * preact) / sharpness).astype(jnp.bfloat16)
    own_batch = batch[:own_rows]
    a_of_b = logical_rank(lat_rank_of(blk ^ me_b, order_b), order_a) ^ me_a
    b_of_a = logical_rank(lat_rank_of(blk ^ me_a, order_a), order_b) ^ me_b
    active_b = take_blocks(active, a_of_b, own_rows)
    halves = []
    for k, (masks, rows) in enumerate(zip(ORDERS, (active, active_b))):
        part = lax.dot_general(
            rows, weight[k * cols:(k + 1) * cols], (((1,), (1,)), ((), ())), preferred_element_type=jnp.float32
        ).astype(jnp.bfloat16)
        halves.append(halving_scatter(part.reshape(n_lat, own_rows, cols), n_lat, masks))
    block_recon = jnp.concatenate(halves, axis=1)
    recon = butterfly_sum(block_recon.astype(jnp.float32), "grp", n_grp, jnp.bfloat16, GRP_MASKS)
    error_own = recon + dec_bias - own_batch.astype(jnp.float32)
    grad_own = (2.0 * error_own).astype(jnp.bfloat16)
    grad_a, grad_b = [g.reshape(n_tok, cols) for g in column_halves(grad_own, n_lat)]
    active_part_b = jnp.dot(grad_b, weight[cols:], preferred_element_type=jnp.float32)
    grad_active = jnp.dot(grad_a, weight[:cols], preferred_element_type=jnp.float32) + take_blocks(
        active_part_b, b_of_a, own_rows
    )
    decoder_grad = jnp.concatenate(
        [
            lax.dot_general(g, a, (((0,), (0,)), ((), ())), preferred_element_type=jnp.float32)
            for g, a in ((grad_a, active), (grad_b, active_b))
        ],
        axis=0,
    )
    grad_pre = (grad_active + penalty) * jax.nn.sigmoid(sharpness * preact)
    encoder_grad = lax.dot_general(
        centered,
        grad_pre.astype(jnp.bfloat16),
        (((0,), (0,)), ((), ())),
        preferred_element_type=jnp.float32,
    )
    grad_raw = encoder_grad + decoder_grad
    bias_raw = jnp.sum(grad_pre, axis=0)
    local_squares = jnp.sum(grad_raw * grad_raw) + jnp.sum(bias_raw * bias_raw)
    squares = jnp.broadcast_to(local_squares, (1, 128))
    for mask in LAT_MASKS:
        squares = squares + lax.ppermute(squares, "lat", masked_pairs(n_lat, mask))
    total_squares = butterfly_sum(squares, "grp", n_grp, jnp.float32, GRP_MASKS)[0, 0]
    entries = (weight.shape[0] + 1) * weight.shape[1] * n_lat * n_grp
    factor = jnp.minimum(1.0, 1.0 / jnp.sqrt(total_squares / entries + epsilon))
    return (
        (grad_raw * factor).astype(jnp.bfloat16),
        bias_raw * factor,
        error_own.astype(jnp.bfloat16),
    )


def solution(mesh):
    return jax.shard_map(
        body,
        mesh=mesh,
        in_specs=(P("lat", None), P(), P(None, ("grp", "lat")), P(("grp", "lat")), P()),
        out_specs=(P(None, ("grp", "lat")), P(("grp", "lat")), P("lat", None)),
        check_vma=False,
    )
```

```python
import jax
import jax.numpy as jnp
import numpy as np
from jax import lax
from jax.sharding import PartitionSpec as P

sharpness = 8.0
penalty = 0.25
epsilon = 1e-06


def butterfly_sum(x, axis, n, send_dtype, masks):
    acc = x
    for mask in masks:
        sent = acc.astype(send_dtype)
        acc = sent.astype(jnp.float32) + lax.ppermute(sent, axis, masked_pairs(n, mask)).astype(jnp.float32)
    return acc


CORE, X1, X3, Y1, Y3 = 1, 2, 6, 8, 24
LAT_MASKS = (CORE, X1, X3, Y1, Y3)
ORDER_X_FIRST = (CORE, X1, X3, Y1, Y3)
ORDER_Y_FIRST = (CORE, X3, X1, Y1, Y3)
ORDERS = (ORDER_X_FIRST, ORDER_Y_FIRST)
GRP_MASKS = (1, 2, 4, 12)


def logical_rank(r, masks):
    coeffs = basis_coefficients(masks)
    out = 0
    for bit in range(5):
        rb = (r >> bit) & 1
        for j in range(5):
            if (coeffs[bit] >> j) & 1:
                out = out ^ (rb << (4 - j))
    return out


def basis_coefficients(masks):
    rows = [(m, 1 << j) for j, m in enumerate(masks)]
    result = []
    for bit in range(5):
        target = 1 << bit
        found = None
        for combo in range(1, 32):
            v = 0
            for j in range(5):
                if (combo >> j) & 1:
                    v ^= rows[j][0]
            if v == target:
                found = combo
                break
        result.append(found)
    return result


def lat_rank_of(p, masks):
    r = 0
    for j, m in enumerate(masks):
        if (p >> (4 - j)) & 1:
            r ^= m
    return r


def masked_pairs(n, mask):
    return [(i, i ^ mask) for i in range(n)]


def halving_rounds(parts, rank, n, orders):
    mes = [logical_rank(rank, masks) for masks in orders]
    accs = list(parts)
    for j in range(len(orders[0])):
        accs = [a.reshape((2, a.shape[0] // 2) + a.shape[1:]) for a in accs]
        bits = [(me >> (4 - j)) & 1 for me in mes]
        kept = [lax.dynamic_index_in_dim(a, b, 0, keepdims=False) for a, b in zip(accs, bits)]
        sent = [lax.dynamic_index_in_dim(a, 1 - b, 0, keepdims=False).astype(jnp.bfloat16) for a, b in zip(accs, bits)]
        masks = [o[j] for o in orders]
        if all(m == masks[0] for m in masks):
            widths = [t.shape[-1] for t in sent]
            got = lax.ppermute(jnp.concatenate(sent, axis=-1), "lat", masked_pairs(n, masks[0]))
            got = jnp.split(got, np.cumsum(widths)[:-1], axis=-1)
        else:
            got = [lax.ppermute(t, "lat", masked_pairs(n, m)) for t, m in zip(sent, masks)]
        accs = [k.astype(jnp.float32) + g.astype(jnp.float32) for k, g in zip(kept, got)]
    return [a[0] for a in accs]


def doubling_rounds(x, rank, n, orders):
    mes = [logical_rank(rank, masks) for masks in orders]
    width = x.shape[1] // len(orders)
    accs = [x[None, :, k * width:(k + 1) * width] for k in range(len(orders))]
    for j in reversed(range(len(orders[0]))):
        masks = [o[j] for o in orders]
        if all(m == masks[0] for m in masks):
            got = lax.ppermute(jnp.concatenate(accs, axis=-1), "lat", masked_pairs(n, masks[0]))
            got = jnp.split(got, len(accs), axis=-1)
        else:
            got = [lax.ppermute(a, "lat", masked_pairs(n, m)) for a, m in zip(accs, masks)]
        new = []
        for a, g, me in zip(accs, got, mes):
            bit = (me >> (4 - j)) & 1
            pair = jnp.stack([a, g])
            new.append(jnp.where(bit == 0, pair, pair[::-1]).reshape((2 * a.shape[0],) + a.shape[1:]))
        accs = new
    return accs


def column_halves(x, rank, n):
    return doubling_rounds(x, rank, n, ORDERS)


def block_perm(src_masks, dst_masks, n):
    return np.array([logical_rank(lat_rank_of(p, dst_masks), src_masks) for p in range(n)], dtype=np.int32)


def take_blocks(x, perm, rows):
    return jnp.take(x.reshape((len(perm), rows) + x.shape[1:]), perm, axis=0).reshape(x.shape)


def body(stream, batch_index, weight, enc_bias, dec_bias):
    own_rows = stream.shape[0]
    n_lat = lax.axis_size("lat")
    n_grp = lax.axis_size("grp")
    rank_lat = lax.axis_index("lat")
    n_tok = batch_index.shape[0]
    cols = weight.shape[0] // 2
    order_a, order_b = ORDERS
    token_of_row = np.array(
        [lat_rank_of(i // own_rows, order_a) * own_rows + i % own_rows for i in range(n_tok)], dtype=np.int32
    )
    src = jnp.take(batch_index, token_of_row)
    stream_halves = column_halves(stream, rank_lat, n_lat)
    batch_halves = []
    for masks, rows in zip(ORDERS, stream_halves):
        place = logical_rank(src // own_rows, masks) * own_rows + src % own_rows
        onehot = (place[:, None] == lax.broadcasted_iota(jnp.int32, (n_tok, n_tok), 1)).astype(rows.dtype)
        batch_halves.append(
            jnp.dot(onehot, rows.reshape(n_tok, cols), preferred_element_type=jnp.float32).astype(jnp.bfloat16)
        )
    batch = jnp.concatenate(batch_halves, axis=1)
    centered = (batch.astype(jnp.float32) - dec_bias).astype(jnp.bfloat16)
    preact = jnp.dot(centered, weight, preferred_element_type=jnp.float32) + enc_bias
    active = (jax.nn.softplus(sharpness * preact) / sharpness).astype(jnp.bfloat16)
    own_block = logical_rank(rank_lat, order_a)
    own_batch = lax.dynamic_slice_in_dim(batch, own_block * own_rows, own_rows, 0)
    active_b = take_blocks(active, block_perm(order_a, order_b, n_lat), own_rows)
    parts = [
        lax.dot_general(
            rows, weight[k * cols:(k + 1) * cols], (((1,), (1,)), ((), ())), preferred_element_type=jnp.float32
        )
        .astype(jnp.bfloat16)
        .reshape(n_lat, own_rows, cols)
        for k, rows in enumerate((active, active_b))
    ]
    block_recon = jnp.concatenate(halving_rounds(parts, rank_lat, n_lat, ORDERS), axis=1)
    recon = butterfly_sum(block_recon.astype(jnp.float32), "grp", n_grp, jnp.bfloat16, GRP_MASKS)
    error_own = recon + dec_bias - own_batch.astype(jnp.float32)
    grad_own = (2.0 * error_own).astype(jnp.bfloat16)
    grad_a, grad_b = [g.reshape(n_tok, cols) for g in column_halves(grad_own, rank_lat, n_lat)]
    active_part_b = jnp.dot(grad_b, weight[cols:], preferred_element_type=jnp.float32)
    grad_active = jnp.dot(grad_a, weight[:cols], preferred_element_type=jnp.float32) + take_blocks(
        active_part_b, block_perm(order_b, order_a, n_lat), own_rows
    )
    decoder_grad = jnp.concatenate(
        [
            lax.dot_general(g, a, (((0,), (0,)), ((), ())), preferred_element_type=jnp.float32)
            for g, a in ((grad_a, active), (grad_b, active_b))
        ],
        axis=0,
    )
    grad_pre = (grad_active + penalty) * jax.nn.sigmoid(sharpness * preact)
    encoder_grad = lax.dot_general(
        centered,
        grad_pre.astype(jnp.bfloat16),
        (((0,), (0,)), ((), ())),
        preferred_element_type=jnp.float32,
    )
    grad_raw = encoder_grad + decoder_grad
    bias_raw = jnp.sum(grad_pre, axis=0)
    local_squares = jnp.sum(grad_raw * grad_raw) + jnp.sum(bias_raw * bias_raw)
    squares = jnp.broadcast_to(local_squares, (1, 128))
    for mask in LAT_MASKS:
        squares = squares + lax.ppermute(squares, "lat", masked_pairs(n_lat, mask))
    total_squares = butterfly_sum(squares, "grp", n_grp, jnp.float32, GRP_MASKS)[0, 0]
    entries = (weight.shape[0] + 1) * weight.shape[1] * n_lat * n_grp
    factor = jnp.minimum(1.0, 1.0 / jnp.sqrt(total_squares / entries + epsilon))
    return (
        (grad_raw * factor).astype(jnp.bfloat16),
        bias_raw * factor,
        error_own.astype(jnp.bfloat16),
    )


def solution(mesh):
    return jax.shard_map(
        body,
        mesh=mesh,
        in_specs=(P("lat", None), P(), P(None, ("grp", "lat")), P(("grp", "lat")), P()),
        out_specs=(P(None, ("grp", "lat")), P(("grp", "lat")), P("lat", None)),
        check_vma=False,
    )
```

```python
import jax
import jax.numpy as jnp
import numpy as np
from jax import lax
from jax.sharding import PartitionSpec as P

sharpness = 8.0
penalty = 0.25
epsilon = 1e-06


def butterfly_sum(x, axis, n, send_dtype, masks):
    acc = x
    for mask in masks:
        sent = acc.astype(send_dtype)
        acc = sent.astype(jnp.float32) + lax.ppermute(sent, axis, masked_pairs(n, mask)).astype(jnp.float32)
    return acc


CORE, X1, X3, Y1, Y3 = 1, 2, 6, 8, 24
LAT_MASKS = (CORE, X1, X3, Y1, Y3)
ORDER_X_FIRST = (CORE, X1, X3, Y1, Y3)
ORDER_Y_FIRST = (CORE, Y1, Y3, X1, X3)
ORDERS = (ORDER_X_FIRST, ORDER_Y_FIRST)
GRP_MASKS = (1, 2, 4, 12)


def logical_rank(r, masks):
    coeffs = basis_coefficients(masks)
    out = 0
    for bit in range(5):
        rb = (r >> bit) & 1
        for j in range(5):
            if (coeffs[bit] >> j) & 1:
                out = out ^ (rb << (4 - j))
    return out


def basis_coefficients(masks):
    rows = [(m, 1 << j) for j, m in enumerate(masks)]
    result = []
    for bit in range(5):
        target = 1 << bit
        found = None
        for combo in range(1, 32):
            v = 0
            for j in range(5):
                if (combo >> j) & 1:
                    v ^= rows[j][0]
            if v == target:
                found = combo
                break
        result.append(found)
    return result


def lat_rank_of(p, masks):
    r = 0
    for j, m in enumerate(masks):
        if (p >> (4 - j)) & 1:
            r ^= m
    return r


def masked_pairs(n, mask):
    return [(i, i ^ mask) for i in range(n)]


def halving_scatter(x, rank, n, masks):
    me = logical_rank(rank, masks)
    acc = x
    for j, mask in enumerate(masks):
        bit = (me >> (4 - j)) & 1
        acc = acc.reshape((2, acc.shape[0] // 2) + acc.shape[1:])
        kept = lax.dynamic_index_in_dim(acc, bit, 0, keepdims=False)
        sent = lax.dynamic_index_in_dim(acc, 1 - bit, 0, keepdims=False).astype(jnp.bfloat16)
        acc = kept.astype(jnp.float32) + lax.ppermute(sent, "lat", masked_pairs(n, mask)).astype(jnp.float32)
    return acc[0]


def doubling_gather(x, rank, n, masks):
    me = logical_rank(rank, masks)
    acc = x[None]
    for j in reversed(range(len(masks))):
        bit = (me >> (4 - j)) & 1
        got = lax.ppermute(acc, "lat", masked_pairs(n, masks[j]))
        pair = jnp.stack([acc, got])
        acc = jnp.where(bit == 0, pair, pair[::-1]).reshape((2 * acc.shape[0],) + acc.shape[1:])
    return acc


def gather_but_last(x, rank, n, masks):
    me = logical_rank(rank, masks)
    acc = x[None]
    for j in reversed(range(1, len(masks))):
        bit = (me >> (4 - j)) & 1
        got = lax.ppermute(acc, "lat", masked_pairs(n, masks[j]))
        pair = jnp.stack([acc, got])
        acc = jnp.where(bit == 0, pair, pair[::-1]).reshape((2 * acc.shape[0],) + acc.shape[1:])
    got = lax.ppermute(acc, "lat", masked_pairs(n, masks[0]))
    return acc, got, (me >> 4) & 1


def by_bit(bit, mine, got):
    pair = jnp.stack([mine, got])
    return jnp.where(bit == 0, pair, pair[::-1]).reshape((2 * mine.shape[0],) + mine.shape[1:])


def column_halves(x, rank, n):
    cols = x.shape[1] // 2
    return [doubling_gather(x[:, k * cols:(k + 1) * cols], rank, n, masks) for k, masks in enumerate(ORDERS)]


def block_perm(src_masks, dst_masks, n):
    return np.array([logical_rank(lat_rank_of(p, dst_masks), src_masks) for p in range(n)], dtype=np.int32)


def take_blocks(x, perm, rows):
    return jnp.take(x.reshape((len(perm), rows) + x.shape[1:]), perm, axis=0).reshape(x.shape)


def body(stream, batch_index, weight, enc_bias, dec_bias):
    own_rows = stream.shape[0]
    n_lat = lax.axis_size("lat")
    n_grp = lax.axis_size("grp")
    rank_lat = lax.axis_index("lat")
    n_tok = batch_index.shape[0]
    cols = weight.shape[0] // 2
    order_a, order_b = ORDERS
    token_of_row = np.array(
        [lat_rank_of(i // own_rows, order_a) * own_rows + i % own_rows for i in range(n_tok)], dtype=np.int32
    )
    src = jnp.take(batch_index, token_of_row)
    stream_halves = column_halves(stream, rank_lat, n_lat)
    batch_halves = []
    for masks, rows in zip(ORDERS, stream_halves):
        place = logical_rank(src // own_rows, masks) * own_rows + src % own_rows
        onehot = (place[:, None] == lax.broadcasted_iota(jnp.int32, (n_tok, n_tok), 1)).astype(rows.dtype)
        batch_halves.append(
            jnp.dot(onehot, rows.reshape(n_tok, cols), preferred_element_type=jnp.float32).astype(jnp.bfloat16)
        )
    batch = jnp.concatenate(batch_halves, axis=1)
    centered = (batch.astype(jnp.float32) - dec_bias).astype(jnp.bfloat16)
    preact = jnp.dot(centered, weight, preferred_element_type=jnp.float32) + enc_bias
    active = (jax.nn.softplus(sharpness * preact) / sharpness).astype(jnp.bfloat16)
    own_block = logical_rank(rank_lat, order_a)
    own_batch = lax.dynamic_slice_in_dim(batch, own_block * own_rows, own_rows, 0)
    active_b = take_blocks(active, block_perm(order_a, order_b, n_lat), own_rows)
    halves = []
    for k, (masks, rows) in enumerate(zip(ORDERS, (active, active_b))):
        part = lax.dot_general(
            rows, weight[k * cols:(k + 1) * cols], (((1,), (1,)), ((), ())), preferred_element_type=jnp.float32
        ).astype(jnp.bfloat16)
        halves.append(halving_scatter(part.reshape(n_lat, own_rows, cols), rank_lat, n_lat, masks))
    block_recon = jnp.concatenate(halves, axis=1)
    recon = butterfly_sum(block_recon.astype(jnp.float32), "grp", n_grp, jnp.bfloat16, GRP_MASKS)
    error_own = recon + dec_bias - own_batch.astype(jnp.float32)
    grad_own = (2.0 * error_own).astype(jnp.bfloat16)
    half_rows = n_tok // 2
    grad_active = None
    decoder_parts = []
    for k, (masks, rows) in enumerate(zip(ORDERS, (active, active_b))):
        mine, got, bit = gather_but_last(grad_own[:, k * cols:(k + 1) * cols], rank_lat, n_lat, masks)
        mine = mine.reshape(half_rows, cols)
        got = got.reshape(half_rows, cols)
        w = weight[k * cols:(k + 1) * cols]
        part = by_bit(
            bit,
            jnp.dot(mine, w, preferred_element_type=jnp.float32),
            jnp.dot(got, w, preferred_element_type=jnp.float32),
        )
        if k == 1:
            part = take_blocks(part, block_perm(order_b, order_a, n_lat), own_rows)
        grad_active = part if grad_active is None else grad_active + part
        own_active = lax.dynamic_slice_in_dim(rows, bit * half_rows, half_rows, 0)
        other_active = lax.dynamic_slice_in_dim(rows, (1 - bit) * half_rows, half_rows, 0)
        decoder_parts.append(
            lax.dot_general(mine, own_active, (((0,), (0,)), ((), ())), preferred_element_type=jnp.float32)
            + lax.dot_general(got, other_active, (((0,), (0,)), ((), ())), preferred_element_type=jnp.float32)
        )
    decoder_grad = jnp.concatenate(decoder_parts, axis=0)
    grad_pre = (grad_active + penalty) * jax.nn.sigmoid(sharpness * preact)
    encoder_grad = lax.dot_general(
        centered,
        grad_pre.astype(jnp.bfloat16),
        (((0,), (0,)), ((), ())),
        preferred_element_type=jnp.float32,
    )
    grad_raw = encoder_grad + decoder_grad
    bias_raw = jnp.sum(grad_pre, axis=0)
    local_squares = jnp.sum(grad_raw * grad_raw) + jnp.sum(bias_raw * bias_raw)
    squares = jnp.broadcast_to(local_squares, (1, 128))
    for mask in LAT_MASKS:
        squares = squares + lax.ppermute(squares, "lat", masked_pairs(n_lat, mask))
    total_squares = butterfly_sum(squares, "grp", n_grp, jnp.float32, GRP_MASKS)[0, 0]
    entries = (weight.shape[0] + 1) * weight.shape[1] * n_lat * n_grp
    factor = jnp.minimum(1.0, 1.0 / jnp.sqrt(total_squares / entries + epsilon))
    return (
        (grad_raw * factor).astype(jnp.bfloat16),
        bias_raw * factor,
        error_own.astype(jnp.bfloat16),
    )


def solution(mesh):
    return jax.shard_map(
        body,
        mesh=mesh,
        in_specs=(P("lat", None), P(), P(None, ("grp", "lat")), P(("grp", "lat")), P()),
        out_specs=(P(None, ("grp", "lat")), P(("grp", "lat")), P("lat", None)),
        check_vma=False,
    )
```

```python
import jax
import jax.numpy as jnp
import numpy as np
from jax import lax
from jax.sharding import PartitionSpec as P

sharpness = 8.0
penalty = 0.25
epsilon = 1e-06


def butterfly_sum(x, axis, n, send_dtype, masks):
    acc = x
    for mask in masks:
        sent = acc.astype(send_dtype)
        acc = sent.astype(jnp.float32) + lax.ppermute(sent, axis, masked_pairs(n, mask)).astype(jnp.float32)
    return acc


CORE, X1, X3, Y1, Y3 = 1, 2, 6, 8, 24
LAT_MASKS = (CORE, X1, X3, Y1, Y3)
ORDER_X_FIRST = (CORE, X1, X3, Y1, Y3)
ORDER_Y_FIRST = (CORE, Y1, Y3, X1, X3)
ORDERS = (ORDER_X_FIRST, ORDER_Y_FIRST)
GRP_MASKS = (1, 2, 4, 12)


def logical_rank(r, masks):
    coeffs = basis_coefficients(masks)
    out = 0
    for bit in range(5):
        rb = (r >> bit) & 1
        for j in range(5):
            if (coeffs[bit] >> j) & 1:
                out = out ^ (rb << (4 - j))
    return out


def basis_coefficients(masks):
    rows = [(m, 1 << j) for j, m in enumerate(masks)]
    result = []
    for bit in range(5):
        target = 1 << bit
        found = None
        for combo in range(1, 32):
            v = 0
            for j in range(5):
                if (combo >> j) & 1:
                    v ^= rows[j][0]
            if v == target:
                found = combo
                break
        result.append(found)
    return result


def lat_rank_of(p, masks):
    r = 0
    for j, m in enumerate(masks):
        if (p >> (4 - j)) & 1:
            r ^= m
    return r


def masked_pairs(n, mask):
    return [(i, i ^ mask) for i in range(n)]


def halving_scatter(x, rank, n, masks):
    me = logical_rank(rank, masks)
    acc = x
    for j, mask in enumerate(masks):
        bit = (me >> (4 - j)) & 1
        acc = acc.reshape((2, acc.shape[0] // 2) + acc.shape[1:])
        kept = lax.dynamic_index_in_dim(acc, bit, 0, keepdims=False)
        sent = lax.dynamic_index_in_dim(acc, 1 - bit, 0, keepdims=False).astype(jnp.bfloat16)
        acc = kept.astype(jnp.float32) + lax.ppermute(sent, "lat", masked_pairs(n, mask)).astype(jnp.float32)
    return acc[0]


def doubling_gather(x, rank, n, masks):
    me = logical_rank(rank, masks)
    acc = x[None]
    for j in reversed(range(len(masks))):
        bit = (me >> (4 - j)) & 1
        got = lax.ppermute(acc, "lat", masked_pairs(n, masks[j]))
        pair = jnp.stack([acc, got])
        acc = jnp.where(bit == 0, pair, pair[::-1]).reshape((2 * acc.shape[0],) + acc.shape[1:])
    return acc


def column_halves(x, rank, n):
    cols = x.shape[1] // 2
    return [doubling_gather(x[:, k * cols:(k + 1) * cols], rank, n, masks) for k, masks in enumerate(ORDERS)]


def block_perm(src_masks, dst_masks, n):
    return np.array([logical_rank(lat_rank_of(p, dst_masks), src_masks) for p in range(n)], dtype=np.int32)


def take_blocks(x, perm, rows):
    return jnp.take(x.reshape((len(perm), rows) + x.shape[1:]), perm, axis=0).reshape(x.shape)


def body(stream, batch_index, weight, enc_bias, dec_bias):
    own_rows = stream.shape[0]
    n_lat = lax.axis_size("lat")
    n_grp = lax.axis_size("grp")
    rank_lat = lax.axis_index("lat")
    n_tok = batch_index.shape[0]
    cols = weight.shape[0] // 2
    order_a, order_b = ORDERS
    token_of_row = np.array(
        [lat_rank_of(i // own_rows, order_a) * own_rows + i % own_rows for i in range(n_tok)], dtype=np.int32
    )
    src = jnp.take(batch_index, token_of_row)
    stream_halves = column_halves(stream, rank_lat, n_lat)
    batch_halves = []
    for masks, rows in zip(ORDERS, stream_halves):
        place = logical_rank(src // own_rows, masks) * own_rows + src % own_rows
        onehot = (place[:, None] == lax.broadcasted_iota(jnp.int32, (n_tok, n_tok), 1)).astype(rows.dtype)
        batch_halves.append(
            jnp.dot(onehot, rows.reshape(n_tok, cols), preferred_element_type=jnp.float32).astype(jnp.bfloat16)
        )
    batch = jnp.concatenate(batch_halves, axis=1)
    centered = (batch.astype(jnp.float32) - dec_bias).astype(jnp.bfloat16)
    preact = jnp.dot(centered, weight, preferred_element_type=jnp.float32) + enc_bias
    active = (jax.nn.softplus(sharpness * preact) / sharpness).astype(jnp.bfloat16)
    own_block = logical_rank(rank_lat, order_a)
    own_batch = lax.dynamic_slice_in_dim(batch, own_block * own_rows, own_rows, 0)
    active_b = take_blocks(active, block_perm(order_a, order_b, n_lat), own_rows)
    halves = []
    for k, (masks, rows) in enumerate(zip(ORDERS, (active, active_b))):
        part = lax.dot_general(
            rows, weight[k * cols:(k + 1) * cols], (((1,), (1,)), ((), ())), preferred_element_type=jnp.float32
        ).astype(jnp.bfloat16)
        halves.append(halving_scatter(part.reshape(n_lat, own_rows, cols), rank_lat, n_lat, masks))
    block_recon = jnp.concatenate(halves, axis=1)
    recon = butterfly_sum(block_recon.astype(jnp.float32), "grp", n_grp, jnp.bfloat16, GRP_MASKS)
    error_own = recon + dec_bias - own_batch.astype(jnp.float32)
    grad_own = (2.0 * error_own).astype(jnp.bfloat16)
    grad_a, grad_b = [g.reshape(n_tok, cols) for g in column_halves(grad_own, rank_lat, n_lat)]
    active_part_b = jnp.dot(grad_b, weight[cols:], preferred_element_type=jnp.float32)
    grad_active = jnp.dot(grad_a, weight[:cols], preferred_element_type=jnp.float32) + take_blocks(
        active_part_b, block_perm(order_b, order_a, n_lat), own_rows
    )
    decoder_grad = jnp.concatenate(
        [
            lax.dot_general(g, a, (((0,), (0,)), ((), ())), preferred_element_type=jnp.float32)
            for g, a in ((grad_a, active), (grad_b, active_b))
        ],
        axis=0,
    )
    grad_pre = (grad_active + penalty) * jax.nn.sigmoid(sharpness * preact)
    encoder_grad = lax.dot_general(
        centered,
        grad_pre.astype(jnp.bfloat16),
        (((0,), (0,)), ((), ())),
        preferred_element_type=jnp.float32,
    )
    grad_raw = lax.optimization_barrier(encoder_grad + decoder_grad)
    bias_raw = jnp.sum(grad_pre, axis=0)
    local_squares = jnp.sum(grad_raw * grad_raw) + jnp.sum(bias_raw * bias_raw)
    squares = jnp.broadcast_to(local_squares, (1, 128))
    for mask in LAT_MASKS:
        squares = squares + lax.ppermute(squares, "lat", masked_pairs(n_lat, mask))
    total_squares = butterfly_sum(squares, "grp", n_grp, jnp.float32, GRP_MASKS)[0, 0]
    entries = (weight.shape[0] + 1) * weight.shape[1] * n_lat * n_grp
    factor = jnp.minimum(1.0, 1.0 / jnp.sqrt(total_squares / entries + epsilon))
    return (
        (grad_raw * factor).astype(jnp.bfloat16),
        bias_raw * factor,
        error_own.astype(jnp.bfloat16),
    )


def solution(mesh):
    return jax.shard_map(
        body,
        mesh=mesh,
        in_specs=(P("lat", None), P(), P(None, ("grp", "lat")), P(("grp", "lat")), P()),
        out_specs=(P(None, ("grp", "lat")), P(("grp", "lat")), P("lat", None)),
        check_vma=False,
    )
```

```python
import jax
import jax.numpy as jnp
import numpy as np
from jax import lax
from jax.sharding import PartitionSpec as P

sharpness = 8.0
penalty = 0.25
epsilon = 1e-06


def butterfly_sum(x, axis, n, send_dtype, masks):
    acc = x
    for mask in masks:
        sent = acc.astype(send_dtype)
        acc = sent.astype(jnp.float32) + lax.ppermute(sent, axis, masked_pairs(n, mask)).astype(jnp.float32)
    return acc


CORE, X1, X3, Y1, Y3 = 1, 2, 6, 8, 24
LAT_MASKS = (CORE, X1, X3, Y1, Y3)
ORDER_X_FIRST = (CORE, X1, X3, Y1, Y3)
ORDER_Y_FIRST = (CORE, Y1, Y3, X1, X3)
ORDERS = (ORDER_X_FIRST, ORDER_Y_FIRST)
GRP_MASKS = (1, 2, 4, 12)


def logical_rank(r, masks):
    coeffs = basis_coefficients(masks)
    out = 0
    for bit in range(5):
        rb = (r >> bit) & 1
        for j in range(5):
            if (coeffs[bit] >> j) & 1:
                out = out ^ (rb << (4 - j))
    return out


def basis_coefficients(masks):
    rows = [(m, 1 << j) for j, m in enumerate(masks)]
    result = []
    for bit in range(5):
        target = 1 << bit
        found = None
        for combo in range(1, 32):
            v = 0
            for j in range(5):
                if (combo >> j) & 1:
                    v ^= rows[j][0]
            if v == target:
                found = combo
                break
        result.append(found)
    return result


def lat_rank_of(p, masks):
    r = 0
    for j, m in enumerate(masks):
        if (p >> (4 - j)) & 1:
            r ^= m
    return r


def masked_pairs(n, mask):
    return [(i, i ^ mask) for i in range(n)]


def halving_scatter(x, rank, n, masks):
    me = logical_rank(rank, masks)
    acc = x
    for j, mask in enumerate(masks):
        bit = (me >> (4 - j)) & 1
        acc = acc.reshape((2, acc.shape[0] // 2) + acc.shape[1:])
        kept = lax.dynamic_index_in_dim(acc, bit, 0, keepdims=False)
        sent = lax.dynamic_index_in_dim(acc, 1 - bit, 0, keepdims=False).astype(jnp.bfloat16)
        acc = kept.astype(jnp.float32) + lax.ppermute(sent, "lat", masked_pairs(n, mask)).astype(jnp.float32)
    return acc[0]


def doubling_gather(x, rank, n, masks):
    me = logical_rank(rank, masks)
    acc = x[None]
    for j in reversed(range(len(masks))):
        bit = (me >> (4 - j)) & 1
        got = lax.ppermute(acc, "lat", masked_pairs(n, masks[j]))
        pair = jnp.stack([acc, got])
        acc = jnp.where(bit == 0, pair, pair[::-1]).reshape((2 * acc.shape[0],) + acc.shape[1:])
    return acc


def column_halves(x, rank, n):
    cols = x.shape[1] // 2
    return [doubling_gather(x[:, k * cols:(k + 1) * cols], rank, n, masks) for k, masks in enumerate(ORDERS)]


def block_perm(src_masks, dst_masks, n):
    return np.array([logical_rank(lat_rank_of(p, dst_masks), src_masks) for p in range(n)], dtype=np.int32)


def take_blocks(x, perm, rows):
    return jnp.take(x.reshape((len(perm), rows) + x.shape[1:]), perm, axis=0).reshape(x.shape)


def body(stream, batch_index, weight, enc_bias, dec_bias):
    own_rows = stream.shape[0]
    n_lat = lax.axis_size("lat")
    n_grp = lax.axis_size("grp")
    rank_lat = lax.axis_index("lat")
    n_tok = batch_index.shape[0]
    cols = weight.shape[0] // 2
    order_a, order_b = ORDERS
    token_of_row = np.array(
        [lat_rank_of(i // own_rows, order_a) * own_rows + i % own_rows for i in range(n_tok)], dtype=np.int32
    )
    src = jnp.take(batch_index, token_of_row)
    stream_halves = column_halves(stream, rank_lat, n_lat)
    batch_halves = []
    for masks, rows in zip(ORDERS, stream_halves):
        place = logical_rank(src // own_rows, masks) * own_rows + src % own_rows
        onehot = (place[:, None] == lax.broadcasted_iota(jnp.int32, (n_tok, n_tok), 1)).astype(rows.dtype)
        batch_halves.append(
            jnp.dot(onehot, rows.reshape(n_tok, cols), preferred_element_type=jnp.float32).astype(jnp.bfloat16)
        )
    batch = jnp.concatenate(batch_halves, axis=1)
    centered = (batch.astype(jnp.float32) - dec_bias).astype(jnp.bfloat16)
    preact = jnp.dot(centered, weight, preferred_element_type=jnp.float32) + enc_bias
    active = (jax.nn.softplus(sharpness * preact) / sharpness).astype(jnp.bfloat16)
    own_block = logical_rank(rank_lat, order_a)
    own_batch = lax.dynamic_slice_in_dim(batch, own_block * own_rows, own_rows, 0)
    own_offset = lax.optimization_barrier(dec_bias - own_batch.astype(jnp.float32))
    active_b = take_blocks(active, block_perm(order_a, order_b, n_lat), own_rows)
    halves = []
    for k, (masks, rows) in enumerate(zip(ORDERS, (active, active_b))):
        part = lax.dot_general(
            rows, weight[k * cols:(k + 1) * cols], (((1,), (1,)), ((), ())), preferred_element_type=jnp.float32
        ).astype(jnp.bfloat16)
        halves.append(halving_scatter(part.reshape(n_lat, own_rows, cols), rank_lat, n_lat, masks))
    block_recon = jnp.concatenate(halves, axis=1)
    recon = butterfly_sum(block_recon.astype(jnp.float32), "grp", n_grp, jnp.bfloat16, GRP_MASKS)
    error_own = recon + own_offset
    grad_own = (2.0 * error_own).astype(jnp.bfloat16)
    grad_a, grad_b = [g.reshape(n_tok, cols) for g in column_halves(grad_own, rank_lat, n_lat)]
    active_part_b = jnp.dot(grad_b, weight[cols:], preferred_element_type=jnp.float32)
    grad_active = jnp.dot(grad_a, weight[:cols], preferred_element_type=jnp.float32) + take_blocks(
        active_part_b, block_perm(order_b, order_a, n_lat), own_rows
    )
    decoder_grad = jnp.concatenate(
        [
            lax.dot_general(g, a, (((0,), (0,)), ((), ())), preferred_element_type=jnp.float32)
            for g, a in ((grad_a, active), (grad_b, active_b))
        ],
        axis=0,
    )
    grad_pre = (grad_active + penalty) * jax.nn.sigmoid(sharpness * preact)
    encoder_grad = lax.dot_general(
        centered,
        grad_pre.astype(jnp.bfloat16),
        (((0,), (0,)), ((), ())),
        preferred_element_type=jnp.float32,
    )
    grad_raw = lax.optimization_barrier(encoder_grad + decoder_grad)
    bias_raw = jnp.sum(grad_pre, axis=0)
    local_squares = jnp.sum(grad_raw * grad_raw) + jnp.sum(bias_raw * bias_raw)
    squares = jnp.broadcast_to(local_squares, (1, 128))
    for mask in LAT_MASKS:
        squares = squares + lax.ppermute(squares, "lat", masked_pairs(n_lat, mask))
    total_squares = butterfly_sum(squares, "grp", n_grp, jnp.float32, GRP_MASKS)[0, 0]
    entries = (weight.shape[0] + 1) * weight.shape[1] * n_lat * n_grp
    factor = jnp.minimum(1.0, 1.0 / jnp.sqrt(total_squares / entries + epsilon))
    return (
        (grad_raw * factor).astype(jnp.bfloat16),
        bias_raw * factor,
        error_own.astype(jnp.bfloat16),
    )


def solution(mesh):
    return jax.shard_map(
        body,
        mesh=mesh,
        in_specs=(P("lat", None), P(), P(None, ("grp", "lat")), P(("grp", "lat")), P()),
        out_specs=(P(None, ("grp", "lat")), P(("grp", "lat")), P("lat", None)),
        check_vma=False,
    )
```

```python
import jax
import jax.numpy as jnp
import numpy as np
from jax import lax
from jax.sharding import PartitionSpec as P

sharpness = 8.0
penalty = 0.25
epsilon = 1e-06


def butterfly_sum(x, axis, n, send_dtype, masks):
    acc = x
    for mask in masks:
        sent = acc.astype(send_dtype)
        acc = sent.astype(jnp.float32) + lax.ppermute(sent, axis, masked_pairs(n, mask)).astype(jnp.float32)
    return acc


CORE, X1, X3, Y1, Y3 = 1, 2, 6, 8, 24
LAT_MASKS = (CORE, X1, X3, Y1, Y3)
ORDER_X_FIRST = (CORE, X1, X3, Y1, Y3)
ORDER_Y_FIRST = (CORE, Y1, Y3, X1, X3)
ORDERS = (ORDER_X_FIRST, ORDER_Y_FIRST)
GRP_MASKS = (1, 2, 4, 12)


def logical_rank(r, masks):
    coeffs = basis_coefficients(masks)
    out = 0
    for bit in range(5):
        rb = (r >> bit) & 1
        for j in range(5):
            if (coeffs[bit] >> j) & 1:
                out = out ^ (rb << (4 - j))
    return out


def basis_coefficients(masks):
    rows = [(m, 1 << j) for j, m in enumerate(masks)]
    result = []
    for bit in range(5):
        target = 1 << bit
        found = None
        for combo in range(1, 32):
            v = 0
            for j in range(5):
                if (combo >> j) & 1:
                    v ^= rows[j][0]
            if v == target:
                found = combo
                break
        result.append(found)
    return result


def lat_rank_of(p, masks):
    r = 0
    for j, m in enumerate(masks):
        if (p >> (4 - j)) & 1:
            r ^= m
    return r


def masked_pairs(n, mask):
    return [(i, i ^ mask) for i in range(n)]


def halving_scatter(x, rank, n, masks):
    me = logical_rank(rank, masks)
    acc = x
    for j, mask in enumerate(masks):
        bit = (me >> (4 - j)) & 1
        acc = acc.reshape((2, acc.shape[0] // 2) + acc.shape[1:])
        kept = lax.dynamic_index_in_dim(acc, bit, 0, keepdims=False)
        sent = lax.dynamic_index_in_dim(acc, 1 - bit, 0, keepdims=False).astype(jnp.bfloat16)
        acc = kept.astype(jnp.float32) + lax.ppermute(sent, "lat", masked_pairs(n, mask)).astype(jnp.float32)
    return acc[0]


def doubling_gather(x, rank, n, masks):
    me = logical_rank(rank, masks)
    acc = x[None]
    for j in reversed(range(len(masks))):
        bit = (me >> (4 - j)) & 1
        got = lax.ppermute(acc, "lat", masked_pairs(n, masks[j]))
        pair = jnp.stack([acc, got])
        acc = jnp.where(bit == 0, pair, pair[::-1]).reshape((2 * acc.shape[0],) + acc.shape[1:])
    return acc


def column_halves(x, rank, n):
    cols = x.shape[1] // 2
    return [doubling_gather(x[:, k * cols:(k + 1) * cols], rank, n, masks) for k, masks in enumerate(ORDERS)]


def block_perm(src_masks, dst_masks, n):
    return np.array([logical_rank(lat_rank_of(p, dst_masks), src_masks) for p in range(n)], dtype=np.int32)


def take_blocks(x, perm, rows):
    return jnp.take(x.reshape((len(perm), rows) + x.shape[1:]), perm, axis=0).reshape(x.shape)


def body(stream, batch_index, weight, enc_bias, dec_bias):
    own_rows = stream.shape[0]
    n_lat = lax.axis_size("lat")
    n_grp = lax.axis_size("grp")
    rank_lat = lax.axis_index("lat")
    n_tok = batch_index.shape[0]
    cols = weight.shape[0] // 2
    order_a, order_b = ORDERS
    token_of_row = np.array(
        [lat_rank_of(i // own_rows, order_a) * own_rows + i % own_rows for i in range(n_tok)], dtype=np.int32
    )
    src = jnp.take(batch_index, token_of_row)
    stream_halves = column_halves(stream, rank_lat, n_lat)
    batch_halves = []
    for masks, rows in zip(ORDERS, stream_halves):
        place = logical_rank(src // own_rows, masks) * own_rows + src % own_rows
        onehot = (place[:, None] == lax.broadcasted_iota(jnp.int32, (n_tok, n_tok), 1)).astype(rows.dtype)
        batch_halves.append(
            jnp.dot(onehot, rows.reshape(n_tok, cols), preferred_element_type=jnp.float32).astype(jnp.bfloat16)
        )
    batch = jnp.concatenate(batch_halves, axis=1)
    centered = (batch.astype(jnp.float32) - dec_bias).astype(jnp.bfloat16)
    preact = jnp.dot(centered, weight, preferred_element_type=jnp.float32) + enc_bias
    active = (jax.nn.softplus(sharpness * preact) / sharpness).astype(jnp.bfloat16)
    own_block = logical_rank(rank_lat, order_a)
    own_batch = lax.dynamic_slice_in_dim(batch, own_block * own_rows, own_rows, 0)
    own_offset = lax.optimization_barrier(dec_bias - own_batch.astype(jnp.float32))
    gate = lax.optimization_barrier(jax.nn.sigmoid(sharpness * preact))
    active_b = take_blocks(active, block_perm(order_a, order_b, n_lat), own_rows)
    halves = []
    for k, (masks, rows) in enumerate(zip(ORDERS, (active, active_b))):
        part = lax.dot_general(
            rows, weight[k * cols:(k + 1) * cols], (((1,), (1,)), ((), ())), preferred_element_type=jnp.float32
        ).astype(jnp.bfloat16)
        halves.append(halving_scatter(part.reshape(n_lat, own_rows, cols), rank_lat, n_lat, masks))
    block_recon = jnp.concatenate(halves, axis=1)
    recon = butterfly_sum(block_recon.astype(jnp.float32), "grp", n_grp, jnp.bfloat16, GRP_MASKS)
    error_own = recon + own_offset
    grad_own = (2.0 * error_own).astype(jnp.bfloat16)
    grad_a, grad_b = [g.reshape(n_tok, cols) for g in column_halves(grad_own, rank_lat, n_lat)]
    active_part_b = jnp.dot(grad_b, weight[cols:], preferred_element_type=jnp.float32)
    grad_active = jnp.dot(grad_a, weight[:cols], preferred_element_type=jnp.float32) + take_blocks(
        active_part_b, block_perm(order_b, order_a, n_lat), own_rows
    )
    decoder_grad = jnp.concatenate(
        [
            lax.dot_general(g, a, (((0,), (0,)), ((), ())), preferred_element_type=jnp.float32)
            for g, a in ((grad_a, active), (grad_b, active_b))
        ],
        axis=0,
    )
    grad_pre = (grad_active + penalty) * gate
    encoder_grad = lax.dot_general(
        centered,
        grad_pre.astype(jnp.bfloat16),
        (((0,), (0,)), ((), ())),
        preferred_element_type=jnp.float32,
    )
    grad_raw = lax.optimization_barrier(encoder_grad + decoder_grad)
    bias_raw = jnp.sum(grad_pre, axis=0)
    local_squares = jnp.sum(grad_raw * grad_raw) + jnp.sum(bias_raw * bias_raw)
    squares = jnp.broadcast_to(local_squares, (1, 128))
    for mask in LAT_MASKS:
        squares = squares + lax.ppermute(squares, "lat", masked_pairs(n_lat, mask))
    total_squares = butterfly_sum(squares, "grp", n_grp, jnp.float32, GRP_MASKS)[0, 0]
    entries = (weight.shape[0] + 1) * weight.shape[1] * n_lat * n_grp
    factor = jnp.minimum(1.0, 1.0 / jnp.sqrt(total_squares / entries + epsilon))
    return (
        (grad_raw * factor).astype(jnp.bfloat16),
        bias_raw * factor,
        error_own.astype(jnp.bfloat16),
    )


def solution(mesh):
    return jax.shard_map(
        body,
        mesh=mesh,
        in_specs=(P("lat", None), P(), P(None, ("grp", "lat")), P(("grp", "lat")), P()),
        out_specs=(P(None, ("grp", "lat")), P(("grp", "lat")), P("lat", None)),
        check_vma=False,
    )
```
